512 devices in a mesh: dom: 16 (over x_hi, y, core), band: 32 (over z, x_lo).
Axes of the slice: x: 4 (x_hi: 2, x_lo: 2; x = x_hi * 2 + x_lo), y: 4, z: 16, core: 2. Of those that a mesh axis runs over, the one named last changes fastest.
Arguments:
- psi: float32 [1024, 192, 2, 384], P('band', 'dom'), may hold values from -6 to 6
- potential: float32 [192, 2, 384], P('dom'), may hold values from -3 to 3
- rotation: bfloat16 [1024, 1024], replicated, may hold values from -0.1875 to 0.1875
Outputs:
- rotated: bfloat16 [1024, 192, 2, 384], P('band', 'dom')
The draws below stay inside these ranges and needn't reach their ends.
All inputs are finite; a program needn't handle non-finite values.
Results may differ from the reference program's by a relative error of at most 0.005.
Values may be sent and summed in bfloat16 or wider, within the bound.
No kernel may reach another device: no remote copies, remote signals or barrier semaphores. Data moves between devices by JAX's collectives and lax.ppermute only.
A program may use at most 128 MiB of HBM per device.

```python
import jax
import jax.numpy as jnp
from jax import lax

STATES = 1024
NZ = 2
NY = 384
NX = 192


def levels(key, dims, cuts, smallest, largest):
    loudness, own = 1.0, jax.random.fold_in(key, 6)
    for dim, parts in cuts:
        heights = jnp.exp(jax.random.uniform(jax.random.fold_in(own, dim), (parts,), jnp.float32, smallest / len(cuts), largest / len(cuts)))
        loudness = loudness * jnp.repeat(heights, dims[dim] // parts).reshape([-1 if axis == dim else 1 for axis in range(len(dims))])
    return loudness


def bell_draw(stream_key, shape, spread, most, cuts=(), kind=jnp.bfloat16):
    factor_of = levels(stream_key, shape, cuts, -0.22, 0.18) if cuts else 1.0
    entries = jax.random.normal(stream_key, shape, jnp.float32) * spread * factor_of
    return jnp.minimum(jnp.maximum(entries, -most), most).astype(kind)


def setup_inputs(seed: int = 0) -> dict:
    splits = jax.random.split(jax.random.key(seed), 4)
    return {
        "psi": bell_draw(splits[0], (STATES, NX, NZ, NY), 1.0, 6.0, ((0, 32), (1, 16)), jnp.float32),
        "potential": jnp.clip(jax.random.uniform(splits[1], (NX, NZ, NY), jnp.float32, -3.0, 3.0) * levels(splits[1], (NX, NZ, NY), ((0, 16),), -0.4, 0.0), -3.0, 3.0),
        "rotation": bell_draw(splits[2], (STATES, STATES), STATES ** -0.5, 0.1875),
    }


coeffs = (-5369.0 / 1800.0, 12.0 / 7.0, -15.0 / 56.0, 10.0 / 189.0, -1.0 / 112.0, 2.0 / 1925.0, -1.0 / 16632.0)
center_shift = 32.5
half_width = 27.5


def apply_ham(extended, pot, width):
    middle = extended[:, 6:6 + width]
    lap = (3.0 * coeffs[0]) * middle
    for k in range(1, 7):
        lap = lap + coeffs[k] * (extended[:, 6 + k:6 + k + width] + extended[:, 6 - k:6 - k + width])
    for k in range(1, 7):
        lap = lap + coeffs[k] * (jnp.roll(middle, -k, axis=3) + jnp.roll(middle, k, axis=3))
    depth = middle.shape[2]
    planes_out = []
    for j in range(depth):
        plane = lap[:, :, j]
        for k in range(1, 7):
            if j + k < depth:
                plane = plane + coeffs[k] * middle[:, :, j + k]
            if j - k >= 0:
                plane = plane + coeffs[k] * middle[:, :, j - k]
        planes_out.append(plane)
    lap = jnp.stack(planes_out, axis=2)
    return -2.0 * lap + pot[None] * middle


def wrap_x(field):
    return jnp.concatenate([field[:, -6:], field, field[:, :6]], axis=1)


def filter_block(block, potential):
    width = block.shape[1]
    first = (apply_ham(wrap_x(block), potential, width) - center_shift * block) / half_width
    second = (2.0 / half_width) * (apply_ham(wrap_x(first), potential, width) - center_shift * first) - block
    return second.astype(jnp.bfloat16)


def reference(psi, potential, rotation):
    blocks = psi.reshape((STATES // 64, 64) + psi.shape[1:])
    second = lax.map(lambda b: filter_block(b, potential), blocks).reshape(psi.shape)
    flat = second.reshape(STATES, -1)
    mixed = lax.dot_general(rotation, flat, (((0,), (0,)), ((), ())), preferred_element_type=jnp.float32)
    return mixed.astype(jnp.bfloat16).reshape(psi.shape)
```

```python
import jax
import jax.numpy as jnp
from jax import lax
from jax.sharding import PartitionSpec as P

coeffs = (
    -5369.0 / 1800.0,
    12.0 / 7.0,
    -15.0 / 56.0,
    10.0 / 189.0,
    -1.0 / 112.0,
    2.0 / 1925.0,
    -1.0 / 16632.0,
)
center_shift = 32.5
half_width = 27.5


def extended_2(cells, sides, width):
    for axis, dim in sides:
        count = lax.axis_size(axis)
        head = lax.slice_in_dim(cells, 0, width, axis=dim)
        tail = lax.slice_in_dim(cells, cells.shape[dim] - width, cells.shape[dim], axis=dim)
        cells = jnp.concatenate(
            [
                lax.ppermute(tail, axis, [(i, (i + 1) % count) for i in range(count)]),
                cells,
                lax.ppermute(head, axis, [((i + 1) % count, i) for i in range(count)]),
            ],
            axis=dim,
        )
    return cells


def apply_ham(extended, pot, width):
    middle = extended[:, 6 : 6 + width]
    lap = 3.0 * coeffs[0] * middle
    for k in range(1, 7):
        lap = lap + coeffs[k] * (
            extended[:, 6 + k : 6 + k + width] + extended[:, 6 - k : 6 - k + width]
        )
    for k in range(1, 7):
        lap = lap + coeffs[k] * (jnp.roll(middle, -k, axis=3) + jnp.roll(middle, k, axis=3))
    depth = middle.shape[2]
    planes_out = []
    for j in range(depth):
        plane = lap[:, :, j]
        for k in range(1, 7):
            if j + k < depth:
                plane = plane + coeffs[k] * middle[:, :, j + k]
            if j - k >= 0:
                plane = plane + coeffs[k] * middle[:, :, j - k]
        planes_out.append(plane)
    lap = jnp.stack(planes_out, axis=2)
    return -2.0 * lap + pot[None] * middle


def plane_rim(field):
    return extended_2(field, (("dom", 1),), 6)


def per_device(psi, potential, rotation):
    planes = psi.shape[1]
    first = (apply_ham(plane_rim(psi), potential, planes) - center_shift * psi) / half_width
    second = (
        2.0 / half_width * (apply_ham(plane_rim(first), potential, planes) - center_shift * first)
        - psi
    )
    filtered = second.astype(jnp.bfloat16)
    own_states = psi.shape[0]
    count = lax.axis_size("band")
    points = filtered.size // own_states
    chunk = points // count
    blocks = filtered.reshape(own_states, count, chunk).transpose(1, 0, 2)
    gathered = lax.all_to_all(blocks, "band", 0, 0, tiled=True)
    mixed = lax.dot_general(
        rotation,
        gathered.reshape(own_states * count, chunk),
        (((0,), (0,)), ((), ())),
        preferred_element_type=jnp.float32,
    ).astype(jnp.bfloat16)
    back = lax.all_to_all(mixed.reshape(count, own_states, chunk), "band", 0, 0, tiled=True)
    result = back.reshape(count, own_states, chunk).transpose(1, 0, 2)
    return result.reshape(psi.shape)


def solution(mesh):
    in_specs = (P("band", "dom", None, None), P("dom", None, None), P())
    out_specs = P("band", "dom", None, None)
    return jax.shard_map(
        per_device, mesh=mesh, in_specs=in_specs, out_specs=out_specs, check_vma=False
    )
```

```python
import jax
import jax.numpy as jnp
from jax import lax
from jax.experimental import pallas as pl
from jax.experimental.pallas import tpu as pltpu
from jax.sharding import PartitionSpec as P

coeffs = (
    -5369.0 / 1800.0,
    12.0 / 7.0,
    -15.0 / 56.0,
    10.0 / 189.0,
    -1.0 / 112.0,
    2.0 / 1925.0,
    -1.0 / 16632.0,
)
center_shift = 32.5
half_width = 27.5
reach = 6
state_block = 8


def rim_rows(rows):
    count = lax.axis_size("dom")
    halo = 2 * reach
    head = rows[:, :halo]
    tail = rows[:, rows.shape[1] - halo :]
    left = lax.ppermute(tail, "dom", [(i, (i + 1) % count) for i in range(count)])
    right = lax.ppermute(head, "dom", [((i + 1) % count, i) for i in range(count)])
    return jnp.concatenate([left, rows, right], axis=1)


def ham_rows(ext_ref, pot, s, rows, ny):
    halo = 2 * reach
    mid = ext_ref[s, pl.ds(halo, rows), :]
    lap = (3.0 * coeffs[0]) * mid
    for k in range(1, 7):
        lap = lap + coeffs[k] * (
            ext_ref[s, pl.ds(halo + 2 * k, rows), :] + ext_ref[s, pl.ds(halo - 2 * k, rows), :]
        )
    for k in range(1, 7):
        lap = lap + coeffs[k] * (pltpu.roll(mid, k, 1) + pltpu.roll(mid, ny - k, 1))
    up = ext_ref[s, pl.ds(halo + 1, rows), :]
    down = ext_ref[s, pl.ds(halo - 1, rows), :]
    even = lax.broadcasted_iota(jnp.int32, (rows, ny), 0) % 2 == 0
    lap = lap + coeffs[1] * jnp.where(even, up, down)
    return -2.0 * lap + pot * mid, mid


def first_kernel(ext_ref, pot_ref, out_ref):
    rows, ny = out_ref.shape[1], out_ref.shape[2]
    pot = pot_ref[...]

    def body(s, carry):
        h, mid = ham_rows(ext_ref, pot, s, rows, ny)
        out_ref[s] = (h - center_shift * mid) / half_width
        return carry

    lax.fori_loop(0, out_ref.shape[0], body, 0)


def second_kernel(ext_ref, psi_ref, pot_ref, out_ref):
    rows, ny = out_ref.shape[1], out_ref.shape[2]
    pot = pot_ref[...]

    def body(s, carry):
        h, mid = ham_rows(ext_ref, pot, s, rows, ny)
        second = 2.0 / half_width * (h - center_shift * mid) - psi_ref[s]
        out_ref[s] = second.astype(out_ref.dtype)
        return carry

    lax.fori_loop(0, out_ref.shape[0], body, 0)


def run_first(ext, pot):
    states, ext_rows, ny = ext.shape
    rows = pot.shape[0]
    sb = state_block
    return pl.pallas_call(
        first_kernel,
        grid=(states // sb,),
        in_specs=[
            pl.BlockSpec((sb, ext_rows, ny), lambda i: (i, 0, 0)),
            pl.BlockSpec((rows, ny), lambda i: (0, 0)),
        ],
        out_specs=pl.BlockSpec((sb, rows, ny), lambda i: (i, 0, 0)),
        out_shape=jax.ShapeDtypeStruct((states, rows, ny), jnp.float32),
    )(ext, pot)


def run_second(ext, psi, pot):
    states, ext_rows, ny = ext.shape
    rows = pot.shape[0]
    sb = state_block
    return pl.pallas_call(
        second_kernel,
        grid=(states // sb,),
        in_specs=[
            pl.BlockSpec((sb, ext_rows, ny), lambda i: (i, 0, 0)),
            pl.BlockSpec((sb, rows, ny), lambda i: (i, 0, 0)),
            pl.BlockSpec((rows, ny), lambda i: (0, 0)),
        ],
        out_specs=pl.BlockSpec((sb, rows, ny), lambda i: (i, 0, 0)),
        out_shape=jax.ShapeDtypeStruct((states, rows, ny), jnp.bfloat16),
    )(ext, psi, pot)


def per_device(psi, potential, rotation):
    own_states, planes, depth, ny = psi.shape
    rows = planes * depth
    psi_rows = psi.reshape(own_states, rows, ny)
    pot_rows = potential.reshape(rows, ny)
    first = run_first(rim_rows(psi_rows), pot_rows)
    filtered = run_second(rim_rows(first), psi_rows, pot_rows)
    count = lax.axis_size("band")
    points = rows * ny
    chunk = points // count
    blocks = filtered.reshape(own_states, count, chunk).transpose(1, 0, 2)
    gathered = lax.all_to_all(blocks, "band", 0, 0, tiled=True)
    mixed = lax.dot_general(
        rotation,
        gathered.reshape(own_states * count, chunk),
        (((0,), (0,)), ((), ())),
        preferred_element_type=jnp.float32,
    ).astype(jnp.bfloat16)
    back = lax.all_to_all(mixed.reshape(count, own_states, chunk), "band", 0, 0, tiled=True)
    result = back.reshape(count, own_states, chunk).transpose(1, 0, 2)
    return result.reshape(psi.shape)


def solution(mesh):
    in_specs = (P("band", "dom", None, None), P("dom", None, None), P())
    out_specs = P("band", "dom", None, None)
    return jax.shard_map(
        per_device, mesh=mesh, in_specs=in_specs, out_specs=out_specs, check_vma=False
    )
```

```python
import jax
import jax.numpy as jnp
from jax import lax
from jax.experimental import pallas as pl
from jax.experimental.pallas import tpu as pltpu
from jax.sharding import PartitionSpec as P

coeffs = (
    -5369.0 / 1800.0,
    12.0 / 7.0,
    -15.0 / 56.0,
    10.0 / 189.0,
    -1.0 / 112.0,
    2.0 / 1925.0,
    -1.0 / 16632.0,
)
center_shift = 32.5
half_width = 27.5
reach = 6
state_block = 8


def swap_rims(head, tail):
    count = lax.axis_size("dom")
    left = lax.ppermute(tail, "dom", [(i, (i + 1) % count) for i in range(count)])
    right = lax.ppermute(head, "dom", [((i + 1) % count, i) for i in range(count)])
    return left, right


def ham_rows(left_ref, mid_ref, right_ref, ext_ref, pot, p, t, rows, ny):
    halo = 2 * reach
    s = 2 * p + t
    ext_ref[pl.ds(0, halo), :] = left_ref[p, pl.ds(t * halo, halo), :]
    ext_ref[pl.ds(halo, rows), :] = mid_ref[s]
    ext_ref[pl.ds(halo + rows, halo), :] = right_ref[p, pl.ds(t * halo, halo), :]
    mid = ext_ref[pl.ds(halo, rows), :]
    lap = (3.0 * coeffs[0]) * mid
    for k in range(1, 7):
        lap = lap + coeffs[k] * (
            ext_ref[pl.ds(halo + 2 * k, rows), :] + ext_ref[pl.ds(halo - 2 * k, rows), :]
        )
    for k in range(1, 7):
        lap = lap + coeffs[k] * (pltpu.roll(mid, k, 1) + pltpu.roll(mid, ny - k, 1))
    up = ext_ref[pl.ds(halo + 1, rows), :]
    down = ext_ref[pl.ds(halo - 1, rows), :]
    even = lax.broadcasted_iota(jnp.int32, (rows, ny), 0) % 2 == 0
    lap = lap + coeffs[1] * jnp.where(even, up, down)
    return -2.0 * lap + pot * mid, mid


def first_kernel(left_ref, mid_ref, right_ref, pot_ref, out_ref, head_ref, tail_ref, ext_ref):
    rows, ny = out_ref.shape[1], out_ref.shape[2]
    halo = 2 * reach
    pot = pot_ref[...]

    def body(p, carry):
        for t in range(2):
            s = 2 * p + t
            h, mid = ham_rows(left_ref, mid_ref, right_ref, ext_ref, pot, p, t, rows, ny)
            out_ref[s] = (h - center_shift * mid) / half_width
            head_ref[p, pl.ds(t * halo, halo), :] = out_ref[s, pl.ds(0, halo), :]
            tail_ref[p, pl.ds(t * halo, halo), :] = out_ref[s, pl.ds(rows - halo, halo), :]
        return carry

    lax.fori_loop(0, out_ref.shape[0] // 2, body, 0)


def second_kernel(left_ref, mid_ref, right_ref, psi_ref, pot_ref, out_ref, ext_ref):
    rows, ny = out_ref.shape[1], out_ref.shape[2]
    pot = pot_ref[...]

    def body(p, carry):
        for t in range(2):
            s = 2 * p + t
            h, mid = ham_rows(left_ref, mid_ref, right_ref, ext_ref, pot, p, t, rows, ny)
            second = 2.0 / half_width * (h - center_shift * mid) - psi_ref[s]
            out_ref[s] = second.astype(out_ref.dtype)
        return carry

    lax.fori_loop(0, out_ref.shape[0] // 2, body, 0)


def run_first(left, mid, right, pot):
    states, rows, ny = mid.shape
    pair_rows = left.shape[1]
    sb = state_block
    rim = pl.BlockSpec((sb // 2, pair_rows, ny), lambda i: (i, 0, 0))
    body = pl.BlockSpec((sb, rows, ny), lambda i: (i, 0, 0))
    return pl.pallas_call(
        first_kernel,
        grid=(states // sb,),
        in_specs=[rim, body, rim, pl.BlockSpec((rows, ny), lambda i: (0, 0))],
        out_specs=[body, rim, rim],
        out_shape=[
            jax.ShapeDtypeStruct((states, rows, ny), jnp.float32),
            jax.ShapeDtypeStruct(left.shape, jnp.float32),
            jax.ShapeDtypeStruct(left.shape, jnp.float32),
        ],
        scratch_shapes=[pltpu.VMEM((rows + 4 * reach, ny), jnp.float32)],
    )(left, mid, right, pot)


def run_second(left, mid, right, psi, pot):
    states, rows, ny = mid.shape
    pair_rows = left.shape[1]
    sb = state_block
    rim = pl.BlockSpec((sb // 2, pair_rows, ny), lambda i: (i, 0, 0))
    body = pl.BlockSpec((sb, rows, ny), lambda i: (i, 0, 0))
    return pl.pallas_call(
        second_kernel,
        grid=(states // sb,),
        in_specs=[rim, body, rim, body, pl.BlockSpec((rows, ny), lambda i: (0, 0))],
        out_specs=body,
        out_shape=jax.ShapeDtypeStruct((states, rows, ny), jnp.bfloat16),
        scratch_shapes=[pltpu.VMEM((rows + 4 * reach, ny), jnp.float32)],
    )(left, mid, right, psi, pot)


def per_device(psi, potential, rotation):
    own_states, planes, depth, ny = psi.shape
    rows = planes * depth
    halo = 2 * reach
    psi_rows = psi.reshape(own_states, rows, ny)
    pot_rows = potential.reshape(rows, ny)
    pairs = (own_states // 2, 2 * halo, ny)
    left, right = swap_rims(
        psi_rows[:, :halo].reshape(pairs), psi_rows[:, rows - halo :].reshape(pairs)
    )
    first, head, tail = run_first(left, psi_rows, right, pot_rows)
    left, right = swap_rims(head, tail)
    filtered = run_second(left, first, right, psi_rows, pot_rows)
    count = lax.axis_size("band")
    chunk = rows * ny // count
    blocks = filtered.reshape(own_states, count, chunk).transpose(1, 0, 2)
    wire = (count, own_states * chunk // ny, ny)
    gathered = lax.all_to_all(blocks.reshape(wire), "band", 0, 0, tiled=True)
    mixed = lax.dot_general(
        rotation,
        gathered.reshape(own_states * count, chunk),
        (((0,), (0,)), ((), ())),
        preferred_element_type=jnp.float32,
    ).astype(jnp.bfloat16)
    back = lax.all_to_all(mixed.reshape(wire), "band", 0, 0, tiled=True)
    result = back.reshape(count, own_states, chunk).transpose(1, 0, 2)
    return result.reshape(psi.shape)


def solution(mesh):
    in_specs = (P("band", "dom", None, None), P("dom", None, None), P())
    out_specs = P("band", "dom", None, None)
    return jax.shard_map(
        per_device, mesh=mesh, in_specs=in_specs, out_specs=out_specs, check_vma=False
    )
```

```python
import jax
import jax.numpy as jnp
from jax import lax
from jax.experimental import pallas as pl
from jax.experimental.pallas import tpu as pltpu
from jax.sharding import PartitionSpec as P

coeffs = (
    -5369.0 / 1800.0,
    12.0 / 7.0,
    -15.0 / 56.0,
    10.0 / 189.0,
    -1.0 / 112.0,
    2.0 / 1925.0,
    -1.0 / 16632.0,
)
center_shift = 32.5
half_width = 27.5
reach = 6
state_block = 8


def swap_rims(head, tail):
    count = lax.axis_size("dom")
    left = lax.ppermute(tail, "dom", [(i, (i + 1) % count) for i in range(count)])
    right = lax.ppermute(head, "dom", [((i + 1) % count, i) for i in range(count)])
    return left, right


def ham_rows(left_ref, mid_ref, right_ref, ext_ref, pot, p, t, rows, ny):
    halo = 2 * reach
    s = 2 * p + t
    ext_ref[pl.ds(0, halo), :] = left_ref[p, pl.ds(t * halo, halo), :]
    ext_ref[pl.ds(halo, rows), :] = mid_ref[s]
    ext_ref[pl.ds(halo + rows, halo), :] = right_ref[p, pl.ds(t * halo, halo), :]
    mid = ext_ref[pl.ds(halo, rows), :]
    lap = (3.0 * coeffs[0]) * mid
    for k in range(1, 7):
        lap = lap + coeffs[k] * (
            ext_ref[pl.ds(halo + 2 * k, rows), :] + ext_ref[pl.ds(halo - 2 * k, rows), :]
        )
    for k in range(1, 7):
        lap = lap + coeffs[k] * (pltpu.roll(mid, k, 1) + pltpu.roll(mid, ny - k, 1))
    up = ext_ref[pl.ds(halo + 1, rows), :]
    down = ext_ref[pl.ds(halo - 1, rows), :]
    even = lax.broadcasted_iota(jnp.int32, (rows, ny), 0) % 2 == 0
    lap = lap + coeffs[1] * jnp.where(even, up, down)
    return -2.0 * lap + pot * mid, mid


def first_kernel(left_ref, mid_ref, right_ref, pot_ref, out_ref, head_ref, tail_ref, ext_ref):
    rows, ny = out_ref.shape[1], out_ref.shape[2]
    halo = 2 * reach
    pot = pot_ref[...]

    def body(p, carry):
        for t in range(2):
            s = 2 * p + t
            h, mid = ham_rows(left_ref, mid_ref, right_ref, ext_ref, pot, p, t, rows, ny)
            out_ref[s] = (h - center_shift * mid) / half_width
            head_ref[p, pl.ds(t * halo, halo), :] = out_ref[s, pl.ds(0, halo), :]
            tail_ref[p, pl.ds(t * halo, halo), :] = out_ref[s, pl.ds(rows - halo, halo), :]
        return carry

    lax.fori_loop(0, out_ref.shape[0] // 2, body, 0)


def second_kernel(left_ref, mid_ref, right_ref, psi_ref, pot_ref, out_ref, ext_ref):
    rows, ny = out_ref.shape[1], out_ref.shape[2]
    pot = pot_ref[...]

    def body(p, carry):
        for t in range(2):
            s = 2 * p + t
            h, mid = ham_rows(left_ref, mid_ref, right_ref, ext_ref, pot, p, t, rows, ny)
            second = 2.0 / half_width * (h - center_shift * mid) - psi_ref[s]
            out_ref[s] = second.astype(out_ref.dtype)
        return carry

    lax.fori_loop(0, out_ref.shape[0] // 2, body, 0)


def run_first(left, mid, right, pot):
    states, rows, ny = mid.shape
    pair_rows = left.shape[1]
    sb = state_block
    rim = pl.BlockSpec((sb // 2, pair_rows, ny), lambda i: (i, 0, 0))
    body = pl.BlockSpec((sb, rows, ny), lambda i: (i, 0, 0))
    return pl.pallas_call(
        first_kernel,
        grid=(states // sb,),
        in_specs=[rim, body, rim, pl.BlockSpec((rows, ny), lambda i: (0, 0))],
        out_specs=[body, rim, rim],
        out_shape=[
            jax.ShapeDtypeStruct((states, rows, ny), jnp.float32),
            jax.ShapeDtypeStruct(left.shape, jnp.float32),
            jax.ShapeDtypeStruct(left.shape, jnp.float32),
        ],
        scratch_shapes=[pltpu.VMEM((rows + 4 * reach, ny), jnp.float32)],
    )(left, mid, right, pot)


def run_second(left, mid, right, psi, pot):
    states, rows, ny = mid.shape
    pair_rows = left.shape[1]
    sb = state_block
    rim = pl.BlockSpec((sb // 2, pair_rows, ny), lambda i: (i, 0, 0))
    body = pl.BlockSpec((sb, rows, ny), lambda i: (i, 0, 0))
    return pl.pallas_call(
        second_kernel,
        grid=(states // sb,),
        in_specs=[rim, body, rim, body, pl.BlockSpec((rows, ny), lambda i: (0, 0))],
        out_specs=body,
        out_shape=jax.ShapeDtypeStruct((states, rows, ny), jnp.bfloat16),
        scratch_shapes=[pltpu.VMEM((rows + 4 * reach, ny), jnp.float32)],
    )(left, mid, right, psi, pot)


def per_device(psi, potential, rotation):
    own_states, planes, depth, ny = psi.shape
    rows = planes * depth
    halo = 2 * reach
    pairs = (own_states // 2, 2 * halo, ny)
    left, right = swap_rims(
        psi[:, :reach].reshape(pairs), psi[:, planes - reach :].reshape(pairs)
    )
    psi_rows = psi.reshape(own_states, rows, ny)
    pot_rows = potential.reshape(rows, ny)
    first, head, tail = run_first(left, psi_rows, right, pot_rows)
    left, right = swap_rims(head, tail)
    filtered = run_second(left, first, right, psi_rows, pot_rows)
    count = lax.axis_size("band")
    chunk = rows * ny // count
    blocks = filtered.reshape(own_states, count, chunk).transpose(1, 0, 2)
    wire = (count, own_states * chunk // ny, ny)
    gathered = lax.all_to_all(blocks.reshape(wire), "band", 0, 0, tiled=True)
    mixed = lax.dot_general(
        rotation,
        gathered.reshape(own_states * count, chunk),
        (((0,), (0,)), ((), ())),
        preferred_element_type=jnp.float32,
    ).astype(jnp.bfloat16)
    back = lax.all_to_all(mixed.reshape(wire), "band", 0, 0, tiled=True)
    result = back.reshape(count, own_states, chunk).transpose(1, 0, 2)
    return result.reshape(psi.shape)


def solution(mesh):
    in_specs = (P("band", "dom", None, None), P("dom", None, None), P())
    out_specs = P("band", "dom", None, None)
    return jax.shard_map(
        per_device, mesh=mesh, in_specs=in_specs, out_specs=out_specs, check_vma=False
    )
```

```python
import jax
import jax.numpy as jnp
from jax import lax
from jax.experimental import pallas as pl
from jax.experimental.pallas import tpu as pltpu
from jax.sharding import PartitionSpec as P

coeffs = (
    -5369.0 / 1800.0,
    12.0 / 7.0,
    -15.0 / 56.0,
    10.0 / 189.0,
    -1.0 / 112.0,
    2.0 / 1925.0,
    -1.0 / 16632.0,
)
center_shift = 32.5
half_width = 27.5
reach = 6
state_block = 8


def swap_rims(head, tail):
    count = lax.axis_size("dom")
    if count % 2:
        left = lax.ppermute(tail, "dom", [(i, (i + 1) % count) for i in range(count)])
        right = lax.ppermute(head, "dom", [((i + 1) % count, i) for i in range(count)])
        return left, right
    even = lax.axis_index("dom") % 2 == 0
    inner = [(i, i + 1) if i % 2 == 0 else (i, i - 1) for i in range(count)]
    outer = [(i, (i - 1) % count) if i % 2 == 0 else (i, (i + 1) % count) for i in range(count)]
    got_inner = lax.ppermute(jnp.where(even, tail, head), "dom", inner)
    got_outer = lax.ppermute(jnp.where(even, head, tail), "dom", outer)
    left = jnp.where(even, got_outer, got_inner)
    right = jnp.where(even, got_inner, got_outer)
    return left, right


def ham_rows(left_ref, mid_ref, right_ref, ext_ref, pot, p, t, rows, ny):
    halo = 2 * reach
    s = 2 * p + t
    ext_ref[pl.ds(0, halo), :] = left_ref[p, pl.ds(t * halo, halo), :]
    ext_ref[pl.ds(halo, rows), :] = mid_ref[s]
    ext_ref[pl.ds(halo + rows, halo), :] = right_ref[p, pl.ds(t * halo, halo), :]
    mid = ext_ref[pl.ds(halo, rows), :]
    lap = (3.0 * coeffs[0]) * mid
    for k in range(1, 7):
        lap = lap + coeffs[k] * (
            ext_ref[pl.ds(halo + 2 * k, rows), :] + ext_ref[pl.ds(halo - 2 * k, rows), :]
        )
    for k in range(1, 7):
        lap = lap + coeffs[k] * (pltpu.roll(mid, k, 1) + pltpu.roll(mid, ny - k, 1))
    up = ext_ref[pl.ds(halo + 1, rows), :]
    down = ext_ref[pl.ds(halo - 1, rows), :]
    even = lax.broadcasted_iota(jnp.int32, (rows, ny), 0) % 2 == 0
    lap = lap + coeffs[1] * jnp.where(even, up, down)
    return -2.0 * lap + pot * mid, mid


def first_kernel(left_ref, mid_ref, right_ref, pot_ref, out_ref, head_ref, tail_ref, ext_ref):
    rows, ny = out_ref.shape[1], out_ref.shape[2]
    halo = 2 * reach
    pot = pot_ref[...]

    def body(p, carry):
        for t in range(2):
            s = 2 * p + t
            h, mid = ham_rows(left_ref, mid_ref, right_ref, ext_ref, pot, p, t, rows, ny)
            out_ref[s] = (h - center_shift * mid) / half_width
            head_ref[p, pl.ds(t * halo, halo), :] = out_ref[s, pl.ds(0, halo), :]
            tail_ref[p, pl.ds(t * halo, halo), :] = out_ref[s, pl.ds(rows - halo, halo), :]
        return carry

    lax.fori_loop(0, out_ref.shape[0] // 2, body, 0)


def second_kernel(left_ref, mid_ref, right_ref, psi_ref, pot_ref, out_ref, ext_ref):
    rows, ny = out_ref.shape[1], out_ref.shape[2]
    pot = pot_ref[...]

    def body(p, carry):
        for t in range(2):
            s = 2 * p + t
            h, mid = ham_rows(left_ref, mid_ref, right_ref, ext_ref, pot, p, t, rows, ny)
            second = 2.0 / half_width * (h - center_shift * mid) - psi_ref[s]
            out_ref[s] = second.astype(out_ref.dtype)
        return carry

    lax.fori_loop(0, out_ref.shape[0] // 2, body, 0)


def run_first(left, mid, right, pot):
    states, rows, ny = mid.shape
    pair_rows = left.shape[1]
    sb = state_block
    rim = pl.BlockSpec((sb // 2, pair_rows, ny), lambda i: (i, 0, 0))
    body = pl.BlockSpec((sb, rows, ny), lambda i: (i, 0, 0))
    return pl.pallas_call(
        first_kernel,
        grid=(states // sb,),
        in_specs=[rim, body, rim, pl.BlockSpec((rows, ny), lambda i: (0, 0))],
        out_specs=[body, rim, rim],
        out_shape=[
            jax.ShapeDtypeStruct((states, rows, ny), jnp.float32),
            jax.ShapeDtypeStruct(left.shape, jnp.float32),
            jax.ShapeDtypeStruct(left.shape, jnp.float32),
        ],
        scratch_shapes=[pltpu.VMEM((rows + 4 * reach, ny), jnp.float32)],
    )(left, mid, right, pot)


def run_second(left, mid, right, psi, pot):
    states, rows, ny = mid.shape
    pair_rows = left.shape[1]
    sb = state_block
    rim = pl.BlockSpec((sb // 2, pair_rows, ny), lambda i: (i, 0, 0))
    body = pl.BlockSpec((sb, rows, ny), lambda i: (i, 0, 0))
    return pl.pallas_call(
        second_kernel,
        grid=(states // sb,),
        in_specs=[rim, body, rim, body, pl.BlockSpec((rows, ny), lambda i: (0, 0))],
        out_specs=body,
        out_shape=jax.ShapeDtypeStruct((states, rows, ny), jnp.bfloat16),
        scratch_shapes=[pltpu.VMEM((rows + 4 * reach, ny), jnp.float32)],
    )(left, mid, right, psi, pot)


def per_device(psi, potential, rotation):
    own_states, planes, depth, ny = psi.shape
    rows = planes * depth
    halo = 2 * reach
    psi_rows = psi.reshape(own_states, rows, ny)
    pot_rows = potential.reshape(rows, ny)
    pairs = (own_states // 2, 2 * halo, ny)
    left, right = swap_rims(
        psi_rows[:, :halo].reshape(pairs), psi_rows[:, rows - halo :].reshape(pairs)
    )
    first, head, tail = run_first(left, psi_rows, right, pot_rows)
    left, right = swap_rims(head, tail)
    filtered = run_second(left, first, right, psi_rows, pot_rows)
    count = lax.axis_size("band")
    chunk = rows * ny // count
    blocks = filtered.reshape(own_states, count, chunk).transpose(1, 0, 2)
    wire = (count, own_states * chunk // ny, ny)
    gathered = lax.all_to_all(blocks.reshape(wire), "band", 0, 0, tiled=True)
    mixed = lax.dot_general(
        rotation,
        gathered.reshape(own_states * count, chunk),
        (((0,), (0,)), ((), ())),
        preferred_element_type=jnp.float32,
    ).astype(jnp.bfloat16)
    back = lax.all_to_all(mixed.reshape(wire), "band", 0, 0, tiled=True)
    result = back.reshape(count, own_states, chunk).transpose(1, 0, 2)
    return result.reshape(psi.shape)


def solution(mesh):
    in_specs = (P("band", "dom", None, None), P("dom", None, None), P())
    out_specs = P("band", "dom", None, None)
    return jax.shard_map(
        per_device, mesh=mesh, in_specs=in_specs, out_specs=out_specs, check_vma=False
    )
```

```python
import jax
import jax.numpy as jnp
from jax import lax
from jax.experimental import pallas as pl
from jax.experimental.pallas import tpu as pltpu
from jax.sharding import PartitionSpec as P

coeffs = (
    -5369.0 / 1800.0,
    12.0 / 7.0,
    -15.0 / 56.0,
    10.0 / 189.0,
    -1.0 / 112.0,
    2.0 / 1925.0,
    -1.0 / 16632.0,
)
center_shift = 32.5
half_width = 27.5
reach = 6
state_block = 8


def swap_rims(head, tail):
    count = lax.axis_size("dom")
    if count % 2:
        left = lax.ppermute(tail, "dom", [(i, (i + 1) % count) for i in range(count)])
        right = lax.ppermute(head, "dom", [((i + 1) % count, i) for i in range(count)])
        return left, right
    even = lax.axis_index("dom") % 2 == 0
    inner = [(i, i + 1) if i % 2 == 0 else (i, i - 1) for i in range(count)]
    outer = [(i, (i - 1) % count) if i % 2 == 0 else (i, (i + 1) % count) for i in range(count)]
    got_inner = lax.ppermute(jnp.where(even, tail, head), "dom", inner)
    got_outer = lax.ppermute(jnp.where(even, head, tail), "dom", outer)
    left = jnp.where(even, got_outer, got_inner)
    right = jnp.where(even, got_inner, got_outer)
    return left, right


def ham_rows(left_ref, mid_ref, right_ref, ext_ref, pot, p, t, rows, ny):
    halo = 2 * reach
    s = 2 * p + t
    ext_ref[pl.ds(0, halo), :] = left_ref[p, pl.ds(t * halo, halo), :]
    ext_ref[pl.ds(halo, rows), :] = mid_ref[s]
    ext_ref[pl.ds(halo + rows, halo), :] = right_ref[p, pl.ds(t * halo, halo), :]
    mid = ext_ref[pl.ds(halo, rows), :]
    lap = (3.0 * coeffs[0]) * mid
    for k in range(1, 7):
        lap = lap + coeffs[k] * (
            ext_ref[pl.ds(halo + 2 * k, rows), :] + ext_ref[pl.ds(halo - 2 * k, rows), :]
        )
    for k in range(1, 7):
        lap = lap + coeffs[k] * (pltpu.roll(mid, k, 1) + pltpu.roll(mid, ny - k, 1))
    up = ext_ref[pl.ds(halo + 1, rows), :]
    down = ext_ref[pl.ds(halo - 1, rows), :]
    even = lax.broadcasted_iota(jnp.int32, (rows, ny), 0) % 2 == 0
    lap = lap + coeffs[1] * jnp.where(even, up, down)
    return -2.0 * lap + pot * mid, mid


def first_kernel(left_ref, mid_ref, right_ref, pot_ref, out_ref, head_ref, tail_ref, ext_ref):
    rows, ny = out_ref.shape[1], out_ref.shape[2]
    halo = 2 * reach
    pot = pot_ref[...]

    def body(p, carry):
        for t in range(2):
            s = 2 * p + t
            h, mid = ham_rows(left_ref, mid_ref, right_ref, ext_ref, pot, p, t, rows, ny)
            out_ref[s] = (h - center_shift * mid) / half_width
            head_ref[p, pl.ds(t * halo, halo), :] = out_ref[s, pl.ds(0, halo), :]
            tail_ref[p, pl.ds(t * halo, halo), :] = out_ref[s, pl.ds(rows - halo, halo), :]
        return carry

    lax.fori_loop(0, out_ref.shape[0] // 2, body, 0)


def second_kernel(left_ref, mid_ref, right_ref, psi_ref, pot_ref, out_ref, ext_ref):
    rows, ny = out_ref.shape[1], out_ref.shape[2]
    pot = pot_ref[...]

    def body(p, carry):
        for t in range(2):
            s = 2 * p + t
            h, mid = ham_rows(left_ref, mid_ref, right_ref, ext_ref, pot, p, t, rows, ny)
            second = 2.0 / half_width * (h - center_shift * mid) - psi_ref[s]
            out_ref[s] = second.astype(out_ref.dtype)
        return carry

    lax.fori_loop(0, out_ref.shape[0] // 2, body, 0)


def run_first(left, mid, right, pot):
    states, rows, ny = mid.shape
    pair_rows = left.shape[1]
    sb = state_block
    rim = pl.BlockSpec((sb // 2, pair_rows, ny), lambda i: (i, 0, 0))
    body = pl.BlockSpec((sb, rows, ny), lambda i: (i, 0, 0))
    return pl.pallas_call(
        first_kernel,
        grid=(states // sb,),
        in_specs=[rim, body, rim, pl.BlockSpec((rows, ny), lambda i: (0, 0))],
        out_specs=[body, rim, rim],
        out_shape=[
            jax.ShapeDtypeStruct((states, rows, ny), jnp.float32),
            jax.ShapeDtypeStruct(left.shape, jnp.float32),
            jax.ShapeDtypeStruct(left.shape, jnp.float32),
        ],
        scratch_shapes=[pltpu.VMEM((rows + 4 * reach, ny), jnp.float32)],
    )(left, mid, right, pot)


def run_second(left, mid, right, psi, pot):
    states, rows, ny = mid.shape
    pair_rows = left.shape[1]
    sb = state_block
    rim = pl.BlockSpec((sb // 2, pair_rows, ny), lambda i: (i, 0, 0))
    body = pl.BlockSpec((sb, rows, ny), lambda i: (i, 0, 0))
    return pl.pallas_call(
        second_kernel,
        grid=(states // sb,),
        in_specs=[rim, body, rim, body, pl.BlockSpec((rows, ny), lambda i: (0, 0))],
        out_specs=body,
        out_shape=jax.ShapeDtypeStruct((states, rows, ny), jnp.bfloat16),
        scratch_shapes=[pltpu.VMEM((rows + 4 * reach, ny), jnp.float32)],
    )(left, mid, right, psi, pot)


def per_device(psi, potential, rotation):
    own_states, planes, depth, ny = psi.shape
    rows = planes * depth
    halo = 2 * reach
    psi_rows = psi.reshape(own_states, rows, ny)
    pot_rows = potential.reshape(rows, ny)
    groups = own_states // (2 * state_block) if own_states % (2 * state_block) == 0 else 1
    size = own_states // groups
    pieces = []
    for g in range(groups):
        part = psi_rows[g * size : (g + 1) * size]
        pairs = (size // 2, 2 * halo, ny)
        left, right = swap_rims(
            part[:, :halo].reshape(pairs), part[:, rows - halo :].reshape(pairs)
        )
        pieces.append((part, left, right))
    firsts = []
    for part, left, right in pieces:
        first, head, tail = run_first(left, part, right, pot_rows)
        firsts.append((part, first, swap_rims(head, tail)))
    filtered = jnp.concatenate(
        [run_second(left, first, right, part, pot_rows) for part, first, (left, right) in firsts],
        axis=0,
    )
    count = lax.axis_size("band")
    chunk = rows * ny // count
    blocks = filtered.reshape(own_states, count, chunk).transpose(1, 0, 2)
    wire = (count, own_states * chunk // ny, ny)
    gathered = lax.all_to_all(blocks.reshape(wire), "band", 0, 0, tiled=True)
    mixed = lax.dot_general(
        rotation,
        gathered.reshape(own_states * count, chunk),
        (((0,), (0,)), ((), ())),
        preferred_element_type=jnp.float32,
    ).astype(jnp.bfloat16)
    back = lax.all_to_all(mixed.reshape(wire), "band", 0, 0, tiled=True)
    result = back.reshape(count, own_states, chunk).transpose(1, 0, 2)
    return result.reshape(psi.shape)


def solution(mesh):
    in_specs = (P("band", "dom", None, None), P("dom", None, None), P())
    out_specs = P("band", "dom", None, None)
    return jax.shard_map(
        per_device, mesh=mesh, in_specs=in_specs, out_specs=out_specs, check_vma=False
    )
```

```python
import jax
import jax.numpy as jnp
from jax import lax
from jax.experimental import pallas as pl
from jax.experimental.pallas import tpu as pltpu
from jax.sharding import PartitionSpec as P

coeffs = (
    -5369.0 / 1800.0,
    12.0 / 7.0,
    -15.0 / 56.0,
    10.0 / 189.0,
    -1.0 / 112.0,
    2.0 / 1925.0,
    -1.0 / 16632.0,
)
center_shift = 32.5
half_width = 27.5
reach = 6
state_block = 8


def swap_rims(head, tail):
    count = lax.axis_size("dom")
    if count % 2:
        left = lax.ppermute(tail, "dom", [(i, (i + 1) % count) for i in range(count)])
        right = lax.ppermute(head, "dom", [((i + 1) % count, i) for i in range(count)])
        return left, right
    even = lax.axis_index("dom") % 2 == 0
    inner = [(i, i + 1) if i % 2 == 0 else (i, i - 1) for i in range(count)]
    outer = [(i, (i - 1) % count) if i % 2 == 0 else (i, (i + 1) % count) for i in range(count)]
    got_inner = lax.ppermute(jnp.where(even, tail, head), "dom", inner)
    got_outer = lax.ppermute(jnp.where(even, head, tail), "dom", outer)
    left = jnp.where(even, got_outer, got_inner)
    right = jnp.where(even, got_inner, got_outer)
    return left, right


def ham_planes(ext_ref, pot_ref, x, z, ny):
    mid = ext_ref[x + reach, z]
    lap = (3.0 * coeffs[0]) * mid
    for k in range(1, 7):
        lap = lap + coeffs[k] * (ext_ref[x + reach + k, z] + ext_ref[x + reach - k, z])
    for k in range(1, 7):
        lap = lap + coeffs[k] * (pltpu.roll(mid, k, 1) + pltpu.roll(mid, ny - k, 1))
    lap = lap + coeffs[1] * ext_ref[x + reach, 1 - z]
    return -2.0 * lap + pot_ref[x, z] * mid, mid


def fill_ext(left_ref, mid_ref, right_ref, ext_ref):
    planes = mid_ref.shape[0]
    ext_ref[pl.ds(0, reach)] = left_ref[...]
    ext_ref[pl.ds(reach, planes)] = mid_ref[...]
    ext_ref[pl.ds(reach + planes, reach)] = right_ref[...]


def first_kernel(left_ref, mid_ref, right_ref, pot_ref, out_ref, head_ref, tail_ref, ext_ref):
    planes, depth, _, ny = out_ref.shape
    fill_ext(left_ref, mid_ref, right_ref, ext_ref)

    def body(x, carry):
        for z in range(depth):
            h, mid = ham_planes(ext_ref, pot_ref, x, z, ny)
            out_ref[x, z] = (h - center_shift * mid) / half_width
        return carry

    lax.fori_loop(0, planes, body, 0)
    head_ref[...] = out_ref[pl.ds(0, reach)]
    tail_ref[...] = out_ref[pl.ds(planes - reach, reach)]


def second_kernel(left_ref, mid_ref, right_ref, psi_ref, pot_ref, out_ref, ext_ref):
    planes, depth, _, ny = out_ref.shape
    fill_ext(left_ref, mid_ref, right_ref, ext_ref)

    def body(x, carry):
        for z in range(depth):
            h, mid = ham_planes(ext_ref, pot_ref, x, z, ny)
            out_ref[x, z] = 2.0 / half_width * (h - center_shift * mid) - psi_ref[x, z]
        return carry

    lax.fori_loop(0, planes, body, 0)


def specs(mid, sb):
    planes, depth, _, ny = mid.shape
    rim = pl.BlockSpec((reach, depth, sb, ny), lambda i: (0, 0, i, 0))
    body = pl.BlockSpec((planes, depth, sb, ny), lambda i: (0, 0, i, 0))
    pot = pl.BlockSpec((planes, depth, 1, ny), lambda i: (0, 0, 0, 0))
    ext = pltpu.VMEM((planes + 2 * reach, depth, sb, ny), jnp.float32)
    return rim, body, pot, ext


def run_first(left, mid, right, pot):
    sb = state_block
    rim, body, pot_spec, ext = specs(mid, sb)
    return pl.pallas_call(
        first_kernel,
        grid=(mid.shape[2] // sb,),
        in_specs=[rim, body, rim, pot_spec],
        out_specs=[body, rim, rim],
        out_shape=[
            jax.ShapeDtypeStruct(mid.shape, jnp.float32),
            jax.ShapeDtypeStruct(left.shape, jnp.float32),
            jax.ShapeDtypeStruct(left.shape, jnp.float32),
        ],
        scratch_shapes=[ext],
    )(left, mid, right, pot)


def run_second(left, mid, right, psi, pot):
    sb = state_block
    rim, body, pot_spec, ext = specs(mid, sb)
    return pl.pallas_call(
        second_kernel,
        grid=(mid.shape[2] // sb,),
        in_specs=[rim, body, rim, body, pot_spec],
        out_specs=body,
        out_shape=jax.ShapeDtypeStruct(mid.shape, jnp.float32),
        scratch_shapes=[ext],
    )(left, mid, right, psi, pot)


def per_device(psi, potential, rotation):
    own_states, planes, depth, ny = psi.shape
    psi_t = psi.transpose(1, 2, 0, 3)
    pot_t = potential[:, :, None, :]
    left, right = swap_rims(psi_t[:reach], psi_t[planes - reach :])
    first, head, tail = run_first(left, psi_t, right, pot_t)
    left, right = swap_rims(head, tail)
    second = run_second(left, first, right, psi_t, pot_t)
    filtered = second.astype(jnp.bfloat16).transpose(2, 0, 1, 3)
    rows = planes * depth
    count = lax.axis_size("band")
    chunk = rows * ny // count
    blocks = filtered.reshape(own_states, count, chunk).transpose(1, 0, 2)
    wire = (count, own_states * chunk // ny, ny)
    gathered = lax.all_to_all(blocks.reshape(wire), "band", 0, 0, tiled=True)
    mixed = lax.dot_general(
        rotation,
        gathered.reshape(own_states * count, chunk),
        (((0,), (0,)), ((), ())),
        preferred_element_type=jnp.float32,
    ).astype(jnp.bfloat16)
    back = lax.all_to_all(mixed.reshape(wire), "band", 0, 0, tiled=True)
    result = back.reshape(count, own_states, chunk).transpose(1, 0, 2)
    return result.reshape(psi.shape)


def solution(mesh):
    in_specs = (P("band", "dom", None, None), P("dom", None, None), P())
    out_specs = P("band", "dom", None, None)
    return jax.shard_map(
        per_device, mesh=mesh, in_specs=in_specs, out_specs=out_specs, check_vma=False
    )
```

```python
import jax
import jax.numpy as jnp
from jax import lax
from jax.experimental import pallas as pl
from jax.experimental.pallas import tpu as pltpu
from jax.sharding import PartitionSpec as P

coeffs = (
    -5369.0 / 1800.0,
    12.0 / 7.0,
    -15.0 / 56.0,
    10.0 / 189.0,
    -1.0 / 112.0,
    2.0 / 1925.0,
    -1.0 / 16632.0,
)
center_shift = 32.5
half_width = 27.5
reach = 6
state_block = 32


def swap_rims(head, tail):
    count = lax.axis_size("dom")
    if count % 2:
        left = lax.ppermute(tail, "dom", [(i, (i + 1) % count) for i in range(count)])
        right = lax.ppermute(head, "dom", [((i + 1) % count, i) for i in range(count)])
        return left, right
    even = lax.axis_index("dom") % 2 == 0
    inner = [(i, i + 1) if i % 2 == 0 else (i, i - 1) for i in range(count)]
    outer = [(i, (i - 1) % count) if i % 2 == 0 else (i, (i + 1) % count) for i in range(count)]
    got_inner = lax.ppermute(jnp.where(even, tail, head), "dom", inner)
    got_outer = lax.ppermute(jnp.where(even, head, tail), "dom", outer)
    left = jnp.where(even, got_outer, got_inner)
    right = jnp.where(even, got_inner, got_outer)
    return left, right


def ham_planes(ext_ref, pot_ref, x, z, ny):
    mid = ext_ref[x + reach, z]
    lap = (3.0 * coeffs[0]) * mid
    for k in range(1, 7):
        lap = lap + coeffs[k] * (ext_ref[x + reach + k, z] + ext_ref[x + reach - k, z])
    for k in range(1, 7):
        lap = lap + coeffs[k] * (pltpu.roll(mid, k, 1) + pltpu.roll(mid, ny - k, 1))
    lap = lap + coeffs[1] * ext_ref[x + reach, 1 - z]
    return -2.0 * lap + pot_ref[x, z] * mid, mid


def fill_ext(left_ref, mid_ref, right_ref, ext_ref):
    planes = mid_ref.shape[0]
    ext_ref[pl.ds(0, reach)] = left_ref[...]
    ext_ref[pl.ds(reach, planes)] = mid_ref[...]
    ext_ref[pl.ds(reach + planes, reach)] = right_ref[...]


def first_kernel(left_ref, mid_ref, right_ref, pot_ref, out_ref, head_ref, tail_ref, ext_ref):
    planes, depth, _, ny = out_ref.shape
    fill_ext(left_ref, mid_ref, right_ref, ext_ref)

    def body(x, carry):
        for z in range(depth):
            h, mid = ham_planes(ext_ref, pot_ref, x, z, ny)
            out_ref[x, z] = (h - center_shift * mid) / half_width
        return carry

    lax.fori_loop(0, planes, body, 0)
    head_ref[...] = out_ref[pl.ds(0, reach)]
    tail_ref[...] = out_ref[pl.ds(planes - reach, reach)]


def second_kernel(left_ref, mid_ref, right_ref, psi_ref, pot_ref, out_ref, ext_ref):
    planes, depth, _, ny = out_ref.shape
    fill_ext(left_ref, mid_ref, right_ref, ext_ref)

    def body(x, carry):
        for z in range(depth):
            h, mid = ham_planes(ext_ref, pot_ref, x, z, ny)
            out_ref[x, z] = 2.0 / half_width * (h - center_shift * mid) - psi_ref[x, z]
        return carry

    lax.fori_loop(0, planes, body, 0)


def specs(mid, sb):
    planes, depth, _, ny = mid.shape
    rim = pl.BlockSpec((reach, depth, sb, ny), lambda i: (0, 0, i, 0))
    body = pl.BlockSpec((planes, depth, sb, ny), lambda i: (0, 0, i, 0))
    pot = pl.BlockSpec((planes, depth, 1, ny), lambda i: (0, 0, 0, 0))
    ext = pltpu.VMEM((planes + 2 * reach, depth, sb, ny), jnp.float32)
    return rim, body, pot, ext


def run_first(left, mid, right, pot):
    sb = state_block
    rim, body, pot_spec, ext = specs(mid, sb)
    return pl.pallas_call(
        first_kernel,
        grid=(mid.shape[2] // sb,),
        in_specs=[rim, body, rim, pot_spec],
        out_specs=[body, rim, rim],
        out_shape=[
            jax.ShapeDtypeStruct(mid.shape, jnp.float32),
            jax.ShapeDtypeStruct(left.shape, jnp.float32),
            jax.ShapeDtypeStruct(left.shape, jnp.float32),
        ],
        scratch_shapes=[ext],
    )(left, mid, right, pot)


def run_second(left, mid, right, psi, pot):
    sb = state_block
    rim, body, pot_spec, ext = specs(mid, sb)
    return pl.pallas_call(
        second_kernel,
        grid=(mid.shape[2] // sb,),
        in_specs=[rim, body, rim, body, pot_spec],
        out_specs=body,
        out_shape=jax.ShapeDtypeStruct(mid.shape, jnp.float32),
        scratch_shapes=[ext],
    )(left, mid, right, psi, pot)


def per_device(psi, potential, rotation):
    own_states, planes, depth, ny = psi.shape
    psi_t = psi.transpose(1, 2, 0, 3)
    pot_t = potential[:, :, None, :]
    left, right = swap_rims(psi_t[:reach], psi_t[planes - reach :])
    first, head, tail = run_first(left, psi_t, right, pot_t)
    left, right = swap_rims(head, tail)
    second = run_second(left, first, right, psi_t, pot_t)
    filtered = second.astype(jnp.bfloat16).transpose(2, 0, 1, 3)
    rows = planes * depth
    count = lax.axis_size("band")
    chunk = rows * ny // count
    blocks = filtered.reshape(own_states, count, chunk).transpose(1, 0, 2)
    wire = (count, own_states * chunk // ny, ny)
    gathered = lax.all_to_all(blocks.reshape(wire), "band", 0, 0, tiled=True)
    mixed = lax.dot_general(
        rotation,
        gathered.reshape(own_states * count, chunk),
        (((0,), (0,)), ((), ())),
        preferred_element_type=jnp.float32,
    ).astype(jnp.bfloat16)
    back = lax.all_to_all(mixed.reshape(wire), "band", 0, 0, tiled=True)
    result = back.reshape(count, own_states, chunk).transpose(1, 0, 2)
    return result.reshape(psi.shape)


def solution(mesh):
    in_specs = (P("band", "dom", None, None), P("dom", None, None), P())
    out_specs = P("band", "dom", None, None)
    return jax.shard_map(
        per_device, mesh=mesh, in_specs=in_specs, out_specs=out_specs, check_vma=False
    )
```

```python
import jax
import jax.numpy as jnp
from jax import lax
from jax.experimental import pallas as pl
from jax.experimental.pallas import tpu as pltpu
from jax.sharding import PartitionSpec as P

coeffs = (
    -5369.0 / 1800.0,
    12.0 / 7.0,
    -15.0 / 56.0,
    10.0 / 189.0,
    -1.0 / 112.0,
    2.0 / 1925.0,
    -1.0 / 16632.0,
)
center_shift = 32.5
half_width = 27.5
reach = 6
state_block = 32


def swap_rims(head, tail):
    count = lax.axis_size("dom")
    if count % 2:
        left = lax.ppermute(tail, "dom", [(i, (i + 1) % count) for i in range(count)])
        right = lax.ppermute(head, "dom", [((i + 1) % count, i) for i in range(count)])
        return left, right
    even = lax.axis_index("dom") % 2 == 0
    inner = [(i, i + 1) if i % 2 == 0 else (i, i - 1) for i in range(count)]
    outer = [(i, (i - 1) % count) if i % 2 == 0 else (i, (i + 1) % count) for i in range(count)]
    got_inner = lax.ppermute(jnp.where(even, tail, head), "dom", inner)
    got_outer = lax.ppermute(jnp.where(even, head, tail), "dom", outer)
    left = jnp.where(even, got_outer, got_inner)
    right = jnp.where(even, got_inner, got_outer)
    return left, right


def ham_planes(ext_ref, pot_ref, x, z, ny):
    mid = ext_ref[x + reach, z]
    lap = (3.0 * coeffs[0]) * mid
    for k in range(1, 7):
        lap = lap + coeffs[k] * (ext_ref[x + reach + k, z] + ext_ref[x + reach - k, z])
    for k in range(1, 7):
        lap = lap + coeffs[k] * (pltpu.roll(mid, k, 1) + pltpu.roll(mid, ny - k, 1))
    lap = lap + coeffs[1] * ext_ref[x + reach, 1 - z]
    return -2.0 * lap + pot_ref[x, z] * mid, mid


def fill_ext(left_ref, mid_ref, right_ref, ext_ref):
    planes = mid_ref.shape[0]
    ext_ref[pl.ds(0, reach)] = left_ref[...]
    ext_ref[pl.ds(reach, planes)] = mid_ref[...]
    ext_ref[pl.ds(reach + planes, reach)] = right_ref[...]


def first_kernel(left_ref, mid_ref, right_ref, pot_ref, out_ref, head_ref, tail_ref, ext_ref):
    planes, depth, _, ny = out_ref.shape
    fill_ext(left_ref, mid_ref, right_ref, ext_ref)

    def body(x, carry):
        for z in range(depth):
            h, mid = ham_planes(ext_ref, pot_ref, x, z, ny)
            out_ref[x, z] = (h - center_shift * mid) / half_width
        return carry

    lax.fori_loop(0, planes, body, 0)
    head_ref[...] = out_ref[pl.ds(0, reach)]
    tail_ref[...] = out_ref[pl.ds(planes - reach, reach)]


def second_kernel(left_ref, mid_ref, right_ref, psi_ref, pot_ref, out_ref, ext_ref):
    planes, depth, _, ny = out_ref.shape
    fill_ext(left_ref, mid_ref, right_ref, ext_ref)

    def body(x, carry):
        for z in range(depth):
            h, mid = ham_planes(ext_ref, pot_ref, x, z, ny)
            out_ref[x, z] = 2.0 / half_width * (h - center_shift * mid) - psi_ref[x, z]
        return carry

    lax.fori_loop(0, planes, body, 0)


def specs(mid, sb):
    planes, depth, _, ny = mid.shape
    rim = pl.BlockSpec((reach, depth, sb, ny), lambda i: (0, 0, i, 0))
    body = pl.BlockSpec((planes, depth, sb, ny), lambda i: (0, 0, i, 0))
    pot = pl.BlockSpec((planes, depth, 1, ny), lambda i: (0, 0, 0, 0))
    ext = pltpu.VMEM((planes + 2 * reach, depth, sb, ny), jnp.float32)
    return rim, body, pot, ext


def run_first(left, mid, right, pot):
    sb = state_block
    rim, body, pot_spec, ext = specs(mid, sb)
    return pl.pallas_call(
        first_kernel,
        grid=(mid.shape[2] // sb,),
        in_specs=[rim, body, rim, pot_spec],
        out_specs=[body, rim, rim],
        out_shape=[
            jax.ShapeDtypeStruct(mid.shape, jnp.float32),
            jax.ShapeDtypeStruct(left.shape, jnp.float32),
            jax.ShapeDtypeStruct(left.shape, jnp.float32),
        ],
        scratch_shapes=[ext],
    )(left, mid, right, pot)


def run_second(left, mid, right, psi, pot):
    sb = state_block
    rim, body, pot_spec, ext = specs(mid, sb)
    return pl.pallas_call(
        second_kernel,
        grid=(mid.shape[2] // sb,),
        in_specs=[rim, body, rim, body, pot_spec],
        out_specs=body,
        out_shape=jax.ShapeDtypeStruct(mid.shape, jnp.float32),
        scratch_shapes=[ext],
    )(left, mid, right, psi, pot)


def first_half_kernel(side_ref, rim_ref, mid_ref, pot_ref, out_ref, ext_ref):
    planes = mid_ref.shape[0]
    depth, ny = out_ref.shape[1], out_ref.shape[3]
    h = side_ref[0]
    ext_ref[pl.ds(reach, planes)] = mid_ref[...]
    ext_ref[pl.ds(h * (reach + planes), reach)] = rim_ref[...]
    base = h * (planes - reach)

    def body(x, carry):
        for z in range(depth):
            hv, mid = ham_planes(ext_ref, pot_ref, base + x, z, ny)
            out_ref[x, z] = (hv - center_shift * mid) / half_width
        return carry

    lax.fori_loop(0, planes - reach, body, 0)


def second_half_kernel(side_ref, rim_ref, a_ref, b_ref, psi_ref, pot_ref, out_ref, ext_ref):
    planes = psi_ref.shape[0]
    half = planes - reach
    depth, ny = out_ref.shape[1], out_ref.shape[3]
    h = side_ref[0]
    a_side = side_ref[1]
    ext_ref[pl.ds(reach + a_side * half, half)] = a_ref[...]
    ext_ref[pl.ds(reach + (1 - a_side) * half, half)] = b_ref[...]
    ext_ref[pl.ds(h * (reach + planes), reach)] = rim_ref[...]
    base = h * half

    def body(x, carry):
        for z in range(depth):
            hv, mid = ham_planes(ext_ref, pot_ref, base + x, z, ny)
            out_ref[x, z] = 2.0 / half_width * (hv - center_shift * mid) - psi_ref[base + x, z]
        return carry

    lax.fori_loop(0, half, body, 0)


def smem():
    return pl.BlockSpec(memory_space=pltpu.SMEM)


def whole(shape):
    return pl.BlockSpec(shape, lambda i: (0,) * len(shape))


def run_first_half(side, rim, mid, pot):
    planes, depth, states, ny = mid.shape
    half = (planes - reach, depth, states, ny)
    return pl.pallas_call(
        first_half_kernel,
        grid=(1,),
        in_specs=[smem(), whole(rim.shape), whole(mid.shape), whole(pot.shape)],
        out_specs=whole(half),
        out_shape=jax.ShapeDtypeStruct(half, jnp.float32),
        scratch_shapes=[pltpu.VMEM((planes + 2 * reach, depth, states, ny), jnp.float32)],
    )(side, rim, mid, pot)


def run_second_half(side, rim, a, b, psi, pot):
    planes, depth, states, ny = psi.shape
    return pl.pallas_call(
        second_half_kernel,
        grid=(1,),
        in_specs=[smem(), whole(rim.shape), whole(a.shape), whole(b.shape), whole(psi.shape), whole(pot.shape)],
        out_specs=whole(a.shape),
        out_shape=jax.ShapeDtypeStruct(a.shape, jnp.float32),
        scratch_shapes=[pltpu.VMEM((planes + 2 * reach, depth, states, ny), jnp.float32)],
    )(side, rim, a, b, psi, pot)


def inner_outer(send_inner, send_outer):
    count = lax.axis_size("dom")
    inner = [(i, i + 1) if i % 2 == 0 else (i, i - 1) for i in range(count)]
    outer = [(i, (i - 1) % count) if i % 2 == 0 else (i, (i + 1) % count) for i in range(count)]
    return lax.ppermute(send_inner, "dom", inner), lax.ppermute(send_outer, "dom", outer)


def per_device(psi, potential, rotation):
    own_states, planes, depth, ny = psi.shape
    psi_t = psi.transpose(1, 2, 0, 3)
    pot_t = potential[:, :, None, :]
    if lax.axis_size("dom") % 2 or planes != 2 * reach:
        left, right = swap_rims(psi_t[:reach], psi_t[planes - reach :])
        first, head, tail = run_first(left, psi_t, right, pot_t)
        left, right = swap_rims(head, tail)
        second = run_second(left, first, right, psi_t, pot_t)
    else:
        even = lax.axis_index("dom") % 2 == 0
        hi = jnp.where(even, 1, 0).astype(jnp.int32)
        head, tail = psi_t[:reach], psi_t[planes - reach :]
        rim_in, rim_out = inner_outer(jnp.where(even, tail, head), jnp.where(even, head, tail))
        part_a = run_first_half(hi.reshape(1), rim_in, psi_t, pot_t)
        part_b = run_first_half((1 - hi).reshape(1), rim_out, psi_t, pot_t)
        rim_in, rim_out = inner_outer(part_a, part_b)
        sides_a = jnp.stack([hi, hi])
        sides_b = jnp.stack([1 - hi, hi])
        second_a = run_second_half(sides_a, rim_in, part_a, part_b, psi_t, pot_t)
        second_b = run_second_half(sides_b, rim_out, part_a, part_b, psi_t, pot_t)
        second = jnp.where(
            even,
            jnp.concatenate([second_b, second_a], axis=0),
            jnp.concatenate([second_a, second_b], axis=0),
        )
    filtered = second.astype(jnp.bfloat16).transpose(2, 0, 1, 3)
    rows = planes * depth
    count = lax.axis_size("band")
    chunk = rows * ny // count
    blocks = filtered.reshape(own_states, count, chunk).transpose(1, 0, 2)
    wire = (count, own_states * chunk // ny, ny)
    gathered = lax.all_to_all(blocks.reshape(wire), "band", 0, 0, tiled=True)
    mixed = lax.dot_general(
        rotation,
        gathered.reshape(own_states * count, chunk),
        (((0,), (0,)), ((), ())),
        preferred_element_type=jnp.float32,
    ).astype(jnp.bfloat16)
    back = lax.all_to_all(mixed.reshape(wire), "band", 0, 0, tiled=True)
    result = back.reshape(count, own_states, chunk).transpose(1, 0, 2)
    return result.reshape(psi.shape)


def solution(mesh):
    in_specs = (P("band", "dom", None, None), P("dom", None, None), P())
    out_specs = P("band", "dom", None, None)
    return jax.shard_map(
        per_device, mesh=mesh, in_specs=in_specs, out_specs=out_specs, check_vma=False
    )
```

```python
import jax
import jax.numpy as jnp
from jax import lax
from jax.experimental import pallas as pl
from jax.experimental.pallas import tpu as pltpu
from jax.sharding import PartitionSpec as P

coeffs = (
    -5369.0 / 1800.0,
    12.0 / 7.0,
    -15.0 / 56.0,
    10.0 / 189.0,
    -1.0 / 112.0,
    2.0 / 1925.0,
    -1.0 / 16632.0,
)
center_shift = 32.5
half_width = 27.5
reach = 6
state_block = 32


def swap_rims(head, tail):
    count = lax.axis_size("dom")
    if count % 2:
        left = lax.ppermute(tail, "dom", [(i, (i + 1) % count) for i in range(count)])
        right = lax.ppermute(head, "dom", [((i + 1) % count, i) for i in range(count)])
        return left, right
    even = lax.axis_index("dom") % 2 == 0
    inner = [(i, i + 1) if i % 2 == 0 else (i, i - 1) for i in range(count)]
    outer = [(i, (i - 1) % count) if i % 2 == 0 else (i, (i + 1) % count) for i in range(count)]
    got_inner = lax.ppermute(jnp.where(even, tail, head), "dom", inner)
    got_outer = lax.ppermute(jnp.where(even, head, tail), "dom", outer)
    left = jnp.where(even, got_outer, got_inner)
    right = jnp.where(even, got_inner, got_outer)
    return left, right


def ham_planes(ext_ref, pot_ref, x, z, ny):
    mid = ext_ref[x + reach, z]
    lap = (3.0 * coeffs[0]) * mid
    for k in range(1, 7):
        lap = lap + coeffs[k] * (ext_ref[x + reach + k, z] + ext_ref[x + reach - k, z])
    for k in range(1, 7):
        lap = lap + coeffs[k] * (pltpu.roll(mid, k, 1) + pltpu.roll(mid, ny - k, 1))
    lap = lap + coeffs[1] * ext_ref[x + reach, 1 - z]
    return -2.0 * lap + pot_ref[x, z] * mid, mid


def fill_ext(left_ref, mid_ref, right_ref, ext_ref):
    planes = mid_ref.shape[0]
    ext_ref[pl.ds(0, reach)] = left_ref[...]
    ext_ref[pl.ds(reach, planes)] = mid_ref[...]
    ext_ref[pl.ds(reach + planes, reach)] = right_ref[...]


def first_kernel(left_ref, mid_ref, right_ref, pot_ref, out_ref, head_ref, tail_ref, ext_ref):
    planes, depth, _, ny = out_ref.shape
    fill_ext(left_ref, mid_ref, right_ref, ext_ref)

    def body(x, carry):
        for z in range(depth):
            h, mid = ham_planes(ext_ref, pot_ref, x, z, ny)
            out_ref[x, z] = (h - center_shift * mid) / half_width
        return carry

    lax.fori_loop(0, planes, body, 0)
    head_ref[...] = out_ref[pl.ds(0, reach)]
    tail_ref[...] = out_ref[pl.ds(planes - reach, reach)]


def second_kernel(left_ref, mid_ref, right_ref, psi_ref, pot_ref, out_ref, ext_ref):
    planes, depth, _, ny = out_ref.shape
    fill_ext(left_ref, mid_ref, right_ref, ext_ref)

    def body(x, carry):
        for z in range(depth):
            h, mid = ham_planes(ext_ref, pot_ref, x, z, ny)
            out_ref[x, z] = 2.0 / half_width * (h - center_shift * mid) - psi_ref[x, z]
        return carry

    lax.fori_loop(0, planes, body, 0)


def specs(mid, sb):
    planes, depth, _, ny = mid.shape
    rim = pl.BlockSpec((reach, depth, sb, ny), lambda i: (0, 0, i, 0))
    body = pl.BlockSpec((planes, depth, sb, ny), lambda i: (0, 0, i, 0))
    pot = pl.BlockSpec((planes, depth, 1, ny), lambda i: (0, 0, 0, 0))
    ext = pltpu.VMEM((planes + 2 * reach, depth, sb, ny), jnp.float32)
    return rim, body, pot, ext


def run_first(left, mid, right, pot):
    sb = state_block
    rim, body, pot_spec, ext = specs(mid, sb)
    return pl.pallas_call(
        first_kernel,
        grid=(mid.shape[2] // sb,),
        in_specs=[rim, body, rim, pot_spec],
        out_specs=[body, rim, rim],
        out_shape=[
            jax.ShapeDtypeStruct(mid.shape, jnp.float32),
            jax.ShapeDtypeStruct(left.shape, jnp.float32),
            jax.ShapeDtypeStruct(left.shape, jnp.float32),
        ],
        scratch_shapes=[ext],
    )(left, mid, right, pot)


def run_second(left, mid, right, psi, pot):
    sb = state_block
    rim, body, pot_spec, ext = specs(mid, sb)
    return pl.pallas_call(
        second_kernel,
        grid=(mid.shape[2] // sb,),
        in_specs=[rim, body, rim, body, pot_spec],
        out_specs=body,
        out_shape=jax.ShapeDtypeStruct(mid.shape, jnp.float32),
        scratch_shapes=[ext],
    )(left, mid, right, psi, pot)


def half_planes(ext_ref, pot_ref, h, base, out_fn, planes):
    depth, ny = ext_ref.shape[1], ext_ref.shape[3]

    def body(x, carry):
        for z in range(depth):
            hv, mid = ham_planes(ext_ref, pot_ref, x, z, ny)
            out_fn(x, z, hv, mid)
        return carry

    lax.fori_loop(0, planes, body, 0)


def rim_terms(ext_ref, xx, z):
    acc = None
    for k in range(1, 7):
        term = coeffs[k] * (ext_ref[xx + reach + k, z] + ext_ref[xx + reach - k, z])
        acc = term if acc is None else acc + term
    return -2.0 * acc


def fill_near(side_ref, rim_ref, mid_ref, ext_ref):
    planes = mid_ref.shape[0]
    h = side_ref[0]
    ext_ref[pl.ds((1 - h) * (reach + planes), reach)] = jnp.zeros(rim_ref.shape, jnp.float32)
    ext_ref[pl.ds(reach, planes)] = mid_ref[...]
    ext_ref[pl.ds(h * (reach + planes), reach)] = rim_ref[...]
    return h


def fill_far(side_ref, rim_ref, ext_ref, planes):
    h = side_ref[0]
    ext_ref[pl.ds((1 - h) * reach, planes + reach)] = jnp.zeros(
        (planes + reach,) + rim_ref.shape[1:], jnp.float32
    )
    ext_ref[pl.ds(h * (reach + planes), reach)] = rim_ref[...]
    return h


def first_near_kernel(side_ref, rim_ref, mid_ref, pot_ref, done_ref, part_ref, ext_ref):
    planes = mid_ref.shape[0]
    half = planes - reach
    h = fill_near(side_ref, rim_ref, mid_ref, ext_ref)
    base = h * half

    def out_fn(x, z, hv, mid):
        mine = (x >= base) & (x < base + half)

        @pl.when(mine)
        def _():
            done_ref[x - base, z] = (hv - center_shift * mid) / half_width

        @pl.when(jnp.logical_not(mine))
        def _():
            part_ref[x - (1 - h) * half, z] = hv

    half_planes(ext_ref, pot_ref, h, base, out_fn, planes)


def first_far_kernel(side_ref, rim_ref, part_ref, mid_ref, out_ref, ext_ref):
    planes = mid_ref.shape[0]
    half = planes - reach
    depth = out_ref.shape[1]
    h = fill_far(side_ref, rim_ref, ext_ref, planes)
    base = h * half

    def body(x, carry):
        for z in range(depth):
            hv = part_ref[x, z] + rim_terms(ext_ref, base + x, z)
            out_ref[x, z] = (hv - center_shift * mid_ref[base + x, z]) / half_width
        return carry

    lax.fori_loop(0, half, body, 0)


def second_near_kernel(side_ref, rim_ref, a_ref, b_ref, psi_ref, pot_ref, done_ref, part_ref, ext_ref):
    planes = psi_ref.shape[0]
    half = planes - reach
    h = side_ref[0]
    a_side = side_ref[1]
    ext_ref[pl.ds((1 - h) * (reach + planes), reach)] = jnp.zeros(rim_ref.shape, jnp.float32)
    ext_ref[pl.ds(reach + a_side * half, half)] = a_ref[...]
    ext_ref[pl.ds(reach + (1 - a_side) * half, half)] = b_ref[...]
    ext_ref[pl.ds(h * (reach + planes), reach)] = rim_ref[...]
    base = h * half

    def out_fn(x, z, hv, mid):
        mine = (x >= base) & (x < base + half)

        @pl.when(mine)
        def _():
            done_ref[x - base, z] = (
                2.0 / half_width * (hv - center_shift * mid) - psi_ref[x, z]
            )

        @pl.when(jnp.logical_not(mine))
        def _():
            part_ref[x - (1 - h) * half, z] = hv

    half_planes(ext_ref, pot_ref, h, base, out_fn, planes)


def second_far_kernel(side_ref, rim_ref, part_ref, a_ref, b_ref, psi_ref, out_ref, ext_ref):
    planes = psi_ref.shape[0]
    half = planes - reach
    depth = out_ref.shape[1]
    h = fill_far(side_ref, rim_ref, ext_ref, planes)
    a_side = side_ref[1]
    base = h * half
    mids = (b_ref, a_ref)

    def body(x, carry):
        for z in range(depth):
            hv = part_ref[x, z] + rim_terms(ext_ref, base + x, z)
            mid = jnp.where(h == a_side, a_ref[x, z], b_ref[x, z])
            out_ref[x, z] = 2.0 / half_width * (hv - center_shift * mid) - psi_ref[base + x, z]
        return carry

    del mids
    lax.fori_loop(0, half, body, 0)


def smem():
    return pl.BlockSpec(memory_space=pltpu.SMEM)


def whole(shape):
    return pl.BlockSpec(shape, lambda i: (0,) * len(shape))


def call(kernel, args, outs, ext_shape):
    specs = [smem()] + [whole(a.shape) for a in args[1:]]
    many = isinstance(outs, list)
    return pl.pallas_call(
        kernel,
        grid=(1,),
        in_specs=specs,
        out_specs=[whole(o) for o in outs] if many else whole(outs),
        out_shape=[jax.ShapeDtypeStruct(o, jnp.float32) for o in outs]
        if many
        else jax.ShapeDtypeStruct(outs, jnp.float32),
        scratch_shapes=[pltpu.VMEM(ext_shape, jnp.float32)],
    )(*args)


def inner_outer(send_inner, send_outer):
    count = lax.axis_size("dom")
    inner = [(i, i + 1) if i % 2 == 0 else (i, i - 1) for i in range(count)]
    outer = [(i, (i - 1) % count) if i % 2 == 0 else (i, (i + 1) % count) for i in range(count)]
    return lax.ppermute(send_inner, "dom", inner), lax.ppermute(send_outer, "dom", outer)


def per_device(psi, potential, rotation):
    own_states, planes, depth, ny = psi.shape
    psi_t = psi.transpose(1, 2, 0, 3)
    pot_t = potential[:, :, None, :]
    if lax.axis_size("dom") % 2 or planes != 2 * reach:
        left, right = swap_rims(psi_t[:reach], psi_t[planes - reach :])
        first, head, tail = run_first(left, psi_t, right, pot_t)
        left, right = swap_rims(head, tail)
        second = run_second(left, first, right, psi_t, pot_t)
    else:
        even = lax.axis_index("dom") % 2 == 0
        hi = jnp.where(even, 1, 0).astype(jnp.int32)
        head, tail = psi_t[:reach], psi_t[planes - reach :]
        rim_in, rim_out = inner_outer(jnp.where(even, tail, head), jnp.where(even, head, tail))
        half = (planes - reach, depth, own_states, ny)
        ext_shape = (planes + 2 * reach, depth, own_states, ny)
        part_a, near_b = call(first_near_kernel, (hi.reshape(1), rim_in, psi_t, pot_t), [half, half], ext_shape)
        part_b = call(first_far_kernel, ((1 - hi).reshape(1), rim_out, near_b, psi_t), half, ext_shape)
        rim_in, rim_out = inner_outer(part_a, part_b)
        sides_a = jnp.stack([hi, hi])
        sides_b = jnp.stack([1 - hi, hi])
        second_a, near_b = call(
            second_near_kernel, (sides_a, rim_in, part_a, part_b, psi_t, pot_t), [half, half], ext_shape
        )
        second_b = call(
            second_far_kernel, (sides_b, rim_out, near_b, part_a, part_b, psi_t), half, ext_shape
        )
        second = jnp.where(
            even,
            jnp.concatenate([second_b, second_a], axis=0),
            jnp.concatenate([second_a, second_b], axis=0),
        )
    filtered = second.astype(jnp.bfloat16).transpose(2, 0, 1, 3)
    rows = planes * depth
    count = lax.axis_size("band")
    chunk = rows * ny // count
    blocks = filtered.reshape(own_states, count, chunk).transpose(1, 0, 2)
    wire = (count, own_states * chunk // ny, ny)
    gathered = lax.all_to_all(blocks.reshape(wire), "band", 0, 0, tiled=True)
    mixed = lax.dot_general(
        rotation,
        gathered.reshape(own_states * count, chunk),
        (((0,), (0,)), ((), ())),
        preferred_element_type=jnp.float32,
    ).astype(jnp.bfloat16)
    back = lax.all_to_all(mixed.reshape(wire), "band", 0, 0, tiled=True)
    result = back.reshape(count, own_states, chunk).transpose(1, 0, 2)
    return result.reshape(psi.shape)


def solution(mesh):
    in_specs = (P("band", "dom", None, None), P("dom", None, None), P())
    out_specs = P("band", "dom", None, None)
    return jax.shard_map(
        per_device, mesh=mesh, in_specs=in_specs, out_specs=out_specs, check_vma=False
    )
```

```python
import jax
import jax.numpy as jnp
from jax import lax
from jax.experimental import pallas as pl
from jax.experimental.pallas import tpu as pltpu
from jax.sharding import PartitionSpec as P

coeffs = (
    -5369.0 / 1800.0,
    12.0 / 7.0,
    -15.0 / 56.0,
    10.0 / 189.0,
    -1.0 / 112.0,
    2.0 / 1925.0,
    -1.0 / 16632.0,
)
center_shift = 32.5
half_width = 27.5
reach = 6
state_block = 32


def swap_rims(head, tail):
    count = lax.axis_size("dom")
    if count % 2:
        left = lax.ppermute(tail, "dom", [(i, (i + 1) % count) for i in range(count)])
        right = lax.ppermute(head, "dom", [((i + 1) % count, i) for i in range(count)])
        return left, right
    even = lax.axis_index("dom") % 2 == 0
    inner = [(i, i + 1) if i % 2 == 0 else (i, i - 1) for i in range(count)]
    outer = [(i, (i - 1) % count) if i % 2 == 0 else (i, (i + 1) % count) for i in range(count)]
    got_inner = lax.ppermute(jnp.where(even, tail, head), "dom", inner)
    got_outer = lax.ppermute(jnp.where(even, head, tail), "dom", outer)
    left = jnp.where(even, got_outer, got_inner)
    right = jnp.where(even, got_inner, got_outer)
    return left, right


def ham_planes(ext_ref, pot_ref, x, z, ny):
    mid = ext_ref[x + reach, z]
    lap = (3.0 * coeffs[0]) * mid
    for k in range(1, 7):
        lap = lap + coeffs[k] * (ext_ref[x + reach + k, z] + ext_ref[x + reach - k, z])
    for k in range(1, 7):
        lap = lap + coeffs[k] * (pltpu.roll(mid, k, 1) + pltpu.roll(mid, ny - k, 1))
    lap = lap + coeffs[1] * ext_ref[x + reach, 1 - z]
    return -2.0 * lap + pot_ref[x, z] * mid, mid


def fill_ext(left_ref, mid_ref, right_ref, ext_ref):
    planes = mid_ref.shape[0]
    ext_ref[pl.ds(0, reach)] = left_ref[...]
    ext_ref[pl.ds(reach, planes)] = mid_ref[...]
    ext_ref[pl.ds(reach + planes, reach)] = right_ref[...]


def first_kernel(left_ref, mid_ref, right_ref, pot_ref, out_ref, head_ref, tail_ref, ext_ref):
    planes, depth, _, ny = out_ref.shape
    fill_ext(left_ref, mid_ref, right_ref, ext_ref)

    def body(x, carry):
        for z in range(depth):
            h, mid = ham_planes(ext_ref, pot_ref, x, z, ny)
            out_ref[x, z] = (h - center_shift * mid) / half_width
        return carry

    lax.fori_loop(0, planes, body, 0)
    head_ref[...] = out_ref[pl.ds(0, reach)]
    tail_ref[...] = out_ref[pl.ds(planes - reach, reach)]


def second_kernel(left_ref, mid_ref, right_ref, psi_ref, pot_ref, out_ref, ext_ref):
    planes, depth, _, ny = out_ref.shape
    fill_ext(left_ref, mid_ref, right_ref, ext_ref)

    def body(x, carry):
        for z in range(depth):
            h, mid = ham_planes(ext_ref, pot_ref, x, z, ny)
            out_ref[x, z] = 2.0 / half_width * (h - center_shift * mid) - psi_ref[x, z]
        return carry

    lax.fori_loop(0, planes, body, 0)


def specs(mid, sb):
    planes, depth, _, ny = mid.shape
    rim = pl.BlockSpec((reach, depth, sb, ny), lambda i: (0, 0, i, 0))
    body = pl.BlockSpec((planes, depth, sb, ny), lambda i: (0, 0, i, 0))
    pot = pl.BlockSpec((planes, depth, 1, ny), lambda i: (0, 0, 0, 0))
    ext = pltpu.VMEM((planes + 2 * reach, depth, sb, ny), jnp.float32)
    return rim, body, pot, ext


def run_first(left, mid, right, pot):
    sb = state_block
    rim, body, pot_spec, ext = specs(mid, sb)
    return pl.pallas_call(
        first_kernel,
        grid=(mid.shape[2] // sb,),
        in_specs=[rim, body, rim, pot_spec],
        out_specs=[body, rim, rim],
        out_shape=[
            jax.ShapeDtypeStruct(mid.shape, jnp.float32),
            jax.ShapeDtypeStruct(left.shape, jnp.float32),
            jax.ShapeDtypeStruct(left.shape, jnp.float32),
        ],
        scratch_shapes=[ext],
    )(left, mid, right, pot)


def run_second(left, mid, right, psi, pot):
    sb = state_block
    rim, body, pot_spec, ext = specs(mid, sb)
    return pl.pallas_call(
        second_kernel,
        grid=(mid.shape[2] // sb,),
        in_specs=[rim, body, rim, body, pot_spec],
        out_specs=body,
        out_shape=jax.ShapeDtypeStruct(mid.shape, jnp.float32),
        scratch_shapes=[ext],
    )(left, mid, right, psi, pot)


def first_half_kernel(side_ref, rim_ref, mid_ref, pot_ref, out_ref, ext_ref):
    planes = mid_ref.shape[0]
    depth, ny = out_ref.shape[1], out_ref.shape[3]
    h = side_ref[0]
    ext_ref[pl.ds(reach, planes)] = mid_ref[...]
    ext_ref[pl.ds(h * (reach + planes), reach)] = rim_ref[...]
    base = h * (planes - reach)

    def body(x, carry):
        for z in range(depth):
            hv, mid = ham_planes(ext_ref, pot_ref, base + x, z, ny)
            out_ref[x, z] = (hv - center_shift * mid) / half_width
        return carry

    lax.fori_loop(0, planes - reach, body, 0)


def second_half_kernel(side_ref, rim_ref, a_ref, b_ref, psi_ref, pot_ref, out_ref, ext_ref):
    planes = psi_ref.shape[0]
    half = planes - reach
    depth, ny = out_ref.shape[1], out_ref.shape[3]
    h = side_ref[0]
    a_side = side_ref[1]
    ext_ref[pl.ds(reach + a_side * half, half)] = a_ref[...]
    ext_ref[pl.ds(reach + (1 - a_side) * half, half)] = b_ref[...]
    ext_ref[pl.ds(h * (reach + planes), reach)] = rim_ref[...]
    base = h * half

    def body(x, carry):
        for z in range(depth):
            hv, mid = ham_planes(ext_ref, pot_ref, base + x, z, ny)
            out_ref[x, z] = 2.0 / half_width * (hv - center_shift * mid) - psi_ref[base + x, z]
        return carry

    lax.fori_loop(0, half, body, 0)


def smem():
    return pl.BlockSpec(memory_space=pltpu.SMEM)


def whole(shape):
    return pl.BlockSpec(shape, lambda i: (0,) * len(shape))


def run_first_half(side, rim, mid, pot):
    planes, depth, states, ny = mid.shape
    half = (planes - reach, depth, states, ny)
    return pl.pallas_call(
        first_half_kernel,
        grid=(1,),
        in_specs=[smem(), whole(rim.shape), whole(mid.shape), whole(pot.shape)],
        out_specs=whole(half),
        out_shape=jax.ShapeDtypeStruct(half, jnp.float32),
        scratch_shapes=[pltpu.VMEM((planes + 2 * reach, depth, states, ny), jnp.float32)],
    )(side, rim, mid, pot)


def run_second_half(side, rim, a, b, psi, pot):
    planes, depth, states, ny = psi.shape
    return pl.pallas_call(
        second_half_kernel,
        grid=(1,),
        in_specs=[smem(), whole(rim.shape), whole(a.shape), whole(b.shape), whole(psi.shape), whole(pot.shape)],
        out_specs=whole(a.shape),
        out_shape=jax.ShapeDtypeStruct(a.shape, jnp.float32),
        scratch_shapes=[pltpu.VMEM((planes + 2 * reach, depth, states, ny), jnp.float32)],
    )(side, rim, a, b, psi, pot)


def inner_outer(send_inner, send_outer):
    count = lax.axis_size("dom")
    inner = [(i, i + 1) if i % 2 == 0 else (i, i - 1) for i in range(count)]
    outer = [(i, (i - 1) % count) if i % 2 == 0 else (i, (i + 1) % count) for i in range(count)]
    return lax.ppermute(send_inner, "dom", inner), lax.ppermute(send_outer, "dom", outer)


def per_device(psi, potential, rotation):
    own_states, planes, depth, ny = psi.shape
    psi_t = psi.transpose(1, 2, 0, 3)
    pot_t = potential[:, :, None, :]
    if lax.axis_size("dom") % 2 or planes != 2 * reach:
        left, right = swap_rims(psi_t[:reach], psi_t[planes - reach :])
        first, head, tail = run_first(left, psi_t, right, pot_t)
        left, right = swap_rims(head, tail)
        second = run_second(left, first, right, psi_t, pot_t)
    else:
        even = lax.axis_index("dom") % 2 == 0
        hi = jnp.where(even, 1, 0).astype(jnp.int32)
        rim_in, rim_out = inner_outer(
            lax.dynamic_slice_in_dim(psi, hi * reach, reach, 1).transpose(1, 2, 0, 3),
            lax.dynamic_slice_in_dim(psi, (1 - hi) * reach, reach, 1).transpose(1, 2, 0, 3),
        )
        part_a = run_first_half(hi.reshape(1), rim_in, psi_t, pot_t)
        part_b = run_first_half((1 - hi).reshape(1), rim_out, psi_t, pot_t)
        rim_in, rim_out = inner_outer(part_a, part_b)
        sides_a = jnp.stack([hi, hi])
        sides_b = jnp.stack([1 - hi, hi])
        second_a = run_second_half(sides_a, rim_in, part_a, part_b, psi_t, pot_t)
        second_b = run_second_half(sides_b, rim_out, part_a, part_b, psi_t, pot_t)
        second = jnp.where(
            even,
            jnp.concatenate([second_b, second_a], axis=0),
            jnp.concatenate([second_a, second_b], axis=0),
        )
    filtered = second.astype(jnp.bfloat16).transpose(2, 0, 1, 3)
    rows = planes * depth
    count = lax.axis_size("band")
    chunk = rows * ny // count
    blocks = filtered.reshape(own_states, count, chunk).transpose(1, 0, 2)
    wire = (count, own_states * chunk // ny, ny)
    gathered = lax.all_to_all(blocks.reshape(wire), "band", 0, 0, tiled=True)
    mixed = lax.dot_general(
        rotation,
        gathered.reshape(own_states * count, chunk),
        (((0,), (0,)), ((), ())),
        preferred_element_type=jnp.float32,
    ).astype(jnp.bfloat16)
    back = lax.all_to_all(mixed.reshape(wire), "band", 0, 0, tiled=True)
    result = back.reshape(count, own_states, chunk).transpose(1, 0, 2)
    return result.reshape(psi.shape)


def solution(mesh):
    in_specs = (P("band", "dom", None, None), P("dom", None, None), P())
    out_specs = P("band", "dom", None, None)
    return jax.shard_map(
        per_device, mesh=mesh, in_specs=in_specs, out_specs=out_specs, check_vma=False
    )
```

```python
import jax
import jax.numpy as jnp
from jax import lax
from jax.experimental import pallas as pl
from jax.experimental.pallas import tpu as pltpu
from jax.sharding import PartitionSpec as P

coeffs = (
    -5369.0 / 1800.0,
    12.0 / 7.0,
    -15.0 / 56.0,
    10.0 / 189.0,
    -1.0 / 112.0,
    2.0 / 1925.0,
    -1.0 / 16632.0,
)
center_shift = 32.5
half_width = 27.5
reach = 6
state_block = 32


def swap_rims(head, tail):
    count = lax.axis_size("dom")
    if count % 2:
        left = lax.ppermute(tail, "dom", [(i, (i + 1) % count) for i in range(count)])
        right = lax.ppermute(head, "dom", [((i + 1) % count, i) for i in range(count)])
        return left, right
    even = lax.axis_index("dom") % 2 == 0
    inner = [(i, i + 1) if i % 2 == 0 else (i, i - 1) for i in range(count)]
    outer = [(i, (i - 1) % count) if i % 2 == 0 else (i, (i + 1) % count) for i in range(count)]
    got_inner = lax.ppermute(jnp.where(even, tail, head), "dom", inner)
    got_outer = lax.ppermute(jnp.where(even, head, tail), "dom", outer)
    left = jnp.where(even, got_outer, got_inner)
    right = jnp.where(even, got_inner, got_outer)
    return left, right


def ham_planes(ext_ref, pot_ref, x, z, ny):
    mid = ext_ref[x + reach, z]
    lap = (3.0 * coeffs[0]) * mid
    for k in range(1, 7):
        lap = lap + coeffs[k] * (ext_ref[x + reach + k, z] + ext_ref[x + reach - k, z])
    for k in range(1, 7):
        lap = lap + coeffs[k] * (pltpu.roll(mid, k, 1) + pltpu.roll(mid, ny - k, 1))
    lap = lap + coeffs[1] * ext_ref[x + reach, 1 - z]
    return -2.0 * lap + pot_ref[x, z] * mid, mid


def fill_ext(left_ref, mid_ref, right_ref, ext_ref):
    planes = mid_ref.shape[0]
    ext_ref[pl.ds(0, reach)] = left_ref[...]
    ext_ref[pl.ds(reach, planes)] = mid_ref[...]
    ext_ref[pl.ds(reach + planes, reach)] = right_ref[...]


def first_kernel(left_ref, mid_ref, right_ref, pot_ref, out_ref, head_ref, tail_ref, ext_ref):
    planes, depth, _, ny = out_ref.shape
    fill_ext(left_ref, mid_ref, right_ref, ext_ref)

    def body(x, carry):
        for z in range(depth):
            h, mid = ham_planes(ext_ref, pot_ref, x, z, ny)
            out_ref[x, z] = (h - center_shift * mid) / half_width
        return carry

    lax.fori_loop(0, planes, body, 0)
    head_ref[...] = out_ref[pl.ds(0, reach)]
    tail_ref[...] = out_ref[pl.ds(planes - reach, reach)]


def second_kernel(left_ref, mid_ref, right_ref, psi_ref, pot_ref, out_ref, ext_ref):
    planes, depth, _, ny = out_ref.shape
    fill_ext(left_ref, mid_ref, right_ref, ext_ref)

    def body(x, carry):
        for z in range(depth):
            h, mid = ham_planes(ext_ref, pot_ref, x, z, ny)
            out_ref[x, z] = 2.0 / half_width * (h - center_shift * mid) - psi_ref[x, z]
        return carry

    lax.fori_loop(0, planes, body, 0)


def specs(mid, sb):
    planes, depth, _, ny = mid.shape
    rim = pl.BlockSpec((reach, depth, sb, ny), lambda i: (0, 0, i, 0))
    body = pl.BlockSpec((planes, depth, sb, ny), lambda i: (0, 0, i, 0))
    pot = pl.BlockSpec((planes, depth, 1, ny), lambda i: (0, 0, 0, 0))
    ext = pltpu.VMEM((planes + 2 * reach, depth, sb, ny), jnp.float32)
    return rim, body, pot, ext


def run_first(left, mid, right, pot):
    sb = state_block
    rim, body, pot_spec, ext = specs(mid, sb)
    return pl.pallas_call(
        first_kernel,
        grid=(mid.shape[2] // sb,),
        in_specs=[rim, body, rim, pot_spec],
        out_specs=[body, rim, rim],
        out_shape=[
            jax.ShapeDtypeStruct(mid.shape, jnp.float32),
            jax.ShapeDtypeStruct(left.shape, jnp.float32),
            jax.ShapeDtypeStruct(left.shape, jnp.float32),
        ],
        scratch_shapes=[ext],
    )(left, mid, right, pot)


def run_second(left, mid, right, psi, pot):
    sb = state_block
    rim, body, pot_spec, ext = specs(mid, sb)
    return pl.pallas_call(
        second_kernel,
        grid=(mid.shape[2] // sb,),
        in_specs=[rim, body, rim, body, pot_spec],
        out_specs=body,
        out_shape=jax.ShapeDtypeStruct(mid.shape, jnp.float32),
        scratch_shapes=[ext],
    )(left, mid, right, psi, pot)


def first_half_kernel(side_ref, rim_ref, mid_ref, pot_ref, out_ref, ext_ref):
    planes = mid_ref.shape[0]
    depth, ny = out_ref.shape[1], out_ref.shape[3]
    h = side_ref[0]
    ext_ref[pl.ds(reach, planes)] = mid_ref[...]
    ext_ref[pl.ds(h * (reach + planes), reach)] = rim_ref[...]
    base = h * (planes - reach)

    def body(x, carry):
        for z in range(depth):
            hv, mid = ham_planes(ext_ref, pot_ref, base + x, z, ny)
            out_ref[x, z] = (hv - center_shift * mid) / half_width
        return carry

    lax.fori_loop(0, planes - reach, body, 0)


def second_half_kernel(side_ref, rim_ref, a_ref, b_ref, psi_ref, pot_ref, out_ref, ext_ref):
    planes = psi_ref.shape[0]
    half = planes - reach
    depth, ny = out_ref.shape[1], out_ref.shape[3]
    h = side_ref[0]
    a_side = side_ref[1]
    ext_ref[pl.ds(reach + a_side * half, half)] = a_ref[...]
    ext_ref[pl.ds(reach + (1 - a_side) * half, half)] = b_ref[...]
    ext_ref[pl.ds(h * (reach + planes), reach)] = rim_ref[...]
    base = h * half

    def body(x, carry):
        for z in range(depth):
            hv, mid = ham_planes(ext_ref, pot_ref, base + x, z, ny)
            out_ref[x, z] = 2.0 / half_width * (hv - center_shift * mid) - psi_ref[base + x, z]
        return carry

    lax.fori_loop(0, half, body, 0)


def smem():
    return pl.BlockSpec(memory_space=pltpu.SMEM)


def whole(shape):
    return pl.BlockSpec(shape, lambda i: (0,) * len(shape))


def run_first_half(side, rim, mid, pot):
    planes, depth, states, ny = mid.shape
    half = (planes - reach, depth, states, ny)
    return pl.pallas_call(
        first_half_kernel,
        grid=(1,),
        in_specs=[smem(), whole(rim.shape), whole(mid.shape), whole(pot.shape)],
        out_specs=whole(half),
        out_shape=jax.ShapeDtypeStruct(half, jnp.float32),
        scratch_shapes=[pltpu.VMEM((planes + 2 * reach, depth, states, ny), jnp.float32)],
    )(side, rim, mid, pot)


def run_second_half(side, rim, a, b, psi, pot):
    planes, depth, states, ny = psi.shape
    return pl.pallas_call(
        second_half_kernel,
        grid=(1,),
        in_specs=[smem(), whole(rim.shape), whole(a.shape), whole(b.shape), whole(psi.shape), whole(pot.shape)],
        out_specs=whole(a.shape),
        out_shape=jax.ShapeDtypeStruct(a.shape, jnp.float32),
        scratch_shapes=[pltpu.VMEM((planes + 2 * reach, depth, states, ny), jnp.float32)],
    )(side, rim, a, b, psi, pot)


def inner_outer(send_inner, send_outer):
    count = lax.axis_size("dom")
    inner = [(i, i + 1) if i % 2 == 0 else (i, i - 1) for i in range(count)]
    outer = [(i, (i - 1) % count) if i % 2 == 0 else (i, (i + 1) % count) for i in range(count)]
    return lax.ppermute(send_inner, "dom", inner), lax.ppermute(send_outer, "dom", outer)


def per_device(psi, potential, rotation):
    own_states, planes, depth, ny = psi.shape
    psi_t = psi.transpose(1, 2, 0, 3)
    pot_t = potential[:, :, None, :]
    if lax.axis_size("dom") % 2 or planes != 2 * reach:
        left, right = swap_rims(psi_t[:reach], psi_t[planes - reach :])
        first, head, tail = run_first(left, psi_t, right, pot_t)
        left, right = swap_rims(head, tail)
        second = run_second(left, first, right, psi_t, pot_t)
    else:
        even = lax.axis_index("dom") % 2 == 0
        hi = jnp.where(even, 1, 0).astype(jnp.int32)
        head, tail = psi_t[:reach], psi_t[planes - reach :]
        rim_in, rim_out = inner_outer(jnp.where(even, tail, head), jnp.where(even, head, tail))
        part_a = run_first_half(hi.reshape(1), rim_in, psi_t, pot_t)
        part_b = run_first_half((1 - hi).reshape(1), rim_out, psi_t, pot_t)
        rim_in, rim_out = inner_outer(part_a, part_b)
        sides_a = jnp.stack([hi, hi])
        sides_b = jnp.stack([1 - hi, hi])
        second_a = run_second_half(sides_a, rim_in, part_a, part_b, psi_t, pot_t)
        second_b = run_second_half(sides_b, rim_out, part_a, part_b, psi_t, pot_t)
        second = jnp.zeros(psi_t.shape, jnp.bfloat16)
        second = lax.dynamic_update_slice_in_dim(second, second_a.astype(jnp.bfloat16), hi * reach, 0)
        second = lax.dynamic_update_slice_in_dim(
            second, second_b.astype(jnp.bfloat16), (1 - hi) * reach, 0
        )
    filtered = second.astype(jnp.bfloat16).transpose(2, 0, 1, 3)
    rows = planes * depth
    count = lax.axis_size("band")
    chunk = rows * ny // count
    blocks = filtered.reshape(own_states, count, chunk).transpose(1, 0, 2)
    wire = (count, own_states * chunk // ny, ny)
    gathered = lax.all_to_all(blocks.reshape(wire), "band", 0, 0, tiled=True)
    mixed = lax.dot_general(
        rotation,
        gathered.reshape(own_states * count, chunk),
        (((0,), (0,)), ((), ())),
        preferred_element_type=jnp.float32,
    ).astype(jnp.bfloat16)
    back = lax.all_to_all(mixed.reshape(wire), "band", 0, 0, tiled=True)
    result = back.reshape(count, own_states, chunk).transpose(1, 0, 2)
    return result.reshape(psi.shape)


def solution(mesh):
    in_specs = (P("band", "dom", None, None), P("dom", None, None), P())
    out_specs = P("band", "dom", None, None)
    return jax.shard_map(
        per_device, mesh=mesh, in_specs=in_specs, out_specs=out_specs, check_vma=False
    )
```

```python
import jax
import jax.numpy as jnp
from jax import lax
from jax.experimental import pallas as pl
from jax.experimental.pallas import tpu as pltpu
from jax.sharding import PartitionSpec as P

coeffs = (
    -5369.0 / 1800.0,
    12.0 / 7.0,
    -15.0 / 56.0,
    10.0 / 189.0,
    -1.0 / 112.0,
    2.0 / 1925.0,
    -1.0 / 16632.0,
)
center_shift = 32.5
half_width = 27.5
reach = 6
state_block = 32


def swap_rims(head, tail):
    count = lax.axis_size("dom")
    if count % 2:
        left = lax.ppermute(tail, "dom", [(i, (i + 1) % count) for i in range(count)])
        right = lax.ppermute(head, "dom", [((i + 1) % count, i) for i in range(count)])
        return left, right
    even = lax.axis_index("dom") % 2 == 0
    inner = [(i, i + 1) if i % 2 == 0 else (i, i - 1) for i in range(count)]
    outer = [(i, (i - 1) % count) if i % 2 == 0 else (i, (i + 1) % count) for i in range(count)]
    got_inner = lax.ppermute(jnp.where(even, tail, head), "dom", inner)
    got_outer = lax.ppermute(jnp.where(even, head, tail), "dom", outer)
    left = jnp.where(even, got_outer, got_inner)
    right = jnp.where(even, got_inner, got_outer)
    return left, right


def ham_planes(ext_ref, pot_ref, x, z, ny):
    mid = ext_ref[x + reach, z]
    lap = (3.0 * coeffs[0]) * mid
    for k in range(1, 7):
        lap = lap + coeffs[k] * (ext_ref[x + reach + k, z] + ext_ref[x + reach - k, z])
    for k in range(1, 7):
        lap = lap + coeffs[k] * (pltpu.roll(mid, k, 1) + pltpu.roll(mid, ny - k, 1))
    lap = lap + coeffs[1] * ext_ref[x + reach, 1 - z]
    return -2.0 * lap + pot_ref[x, z] * mid, mid


def fill_ext(left_ref, mid_ref, right_ref, ext_ref):
    planes = mid_ref.shape[0]
    ext_ref[pl.ds(0, reach)] = left_ref[...]
    ext_ref[pl.ds(reach, planes)] = mid_ref[...]
    ext_ref[pl.ds(reach + planes, reach)] = right_ref[...]


def first_kernel(left_ref, mid_ref, right_ref, pot_ref, out_ref, head_ref, tail_ref, ext_ref):
    planes, depth, _, ny = out_ref.shape
    fill_ext(left_ref, mid_ref, right_ref, ext_ref)

    def body(x, carry):
        for z in range(depth):
            h, mid = ham_planes(ext_ref, pot_ref, x, z, ny)
            out_ref[x, z] = (h - center_shift * mid) / half_width
        return carry

    lax.fori_loop(0, planes, body, 0)
    head_ref[...] = out_ref[pl.ds(0, reach)]
    tail_ref[...] = out_ref[pl.ds(planes - reach, reach)]


def second_kernel(left_ref, mid_ref, right_ref, psi_ref, pot_ref, out_ref, ext_ref):
    planes, depth, _, ny = out_ref.shape
    fill_ext(left_ref, mid_ref, right_ref, ext_ref)

    def body(x, carry):
        for z in range(depth):
            h, mid = ham_planes(ext_ref, pot_ref, x, z, ny)
            out_ref[x, z] = 2.0 / half_width * (h - center_shift * mid) - psi_ref[x, z]
        return carry

    lax.fori_loop(0, planes, body, 0)


def specs(mid, sb):
    planes, depth, _, ny = mid.shape
    rim = pl.BlockSpec((reach, depth, sb, ny), lambda i: (0, 0, i, 0))
    body = pl.BlockSpec((planes, depth, sb, ny), lambda i: (0, 0, i, 0))
    pot = pl.BlockSpec((planes, depth, 1, ny), lambda i: (0, 0, 0, 0))
    ext = pltpu.VMEM((planes + 2 * reach, depth, sb, ny), jnp.float32)
    return rim, body, pot, ext


def run_first(left, mid, right, pot):
    sb = state_block
    rim, body, pot_spec, ext = specs(mid, sb)
    return pl.pallas_call(
        first_kernel,
        grid=(mid.shape[2] // sb,),
        in_specs=[rim, body, rim, pot_spec],
        out_specs=[body, rim, rim],
        out_shape=[
            jax.ShapeDtypeStruct(mid.shape, jnp.float32),
            jax.ShapeDtypeStruct(left.shape, jnp.float32),
            jax.ShapeDtypeStruct(left.shape, jnp.float32),
        ],
        scratch_shapes=[ext],
    )(left, mid, right, pot)


def run_second(left, mid, right, psi, pot):
    sb = state_block
    rim, body, pot_spec, ext = specs(mid, sb)
    return pl.pallas_call(
        second_kernel,
        grid=(mid.shape[2] // sb,),
        in_specs=[rim, body, rim, body, pot_spec],
        out_specs=body,
        out_shape=jax.ShapeDtypeStruct(mid.shape, jnp.float32),
        scratch_shapes=[ext],
    )(left, mid, right, psi, pot)


def first_half_kernel(side_ref, rim_ref, mid_ref, pot_ref, out_ref, ext_ref):
    planes = mid_ref.shape[0]
    depth, ny = out_ref.shape[1], out_ref.shape[3]
    h = side_ref[0]
    ext_ref[pl.ds(reach, planes)] = mid_ref[...]
    ext_ref[pl.ds(h * (reach + planes), reach)] = rim_ref[...]
    base = h * (planes - reach)

    def body(x, carry):
        for z in range(depth):
            hv, mid = ham_planes(ext_ref, pot_ref, base + x, z, ny)
            out_ref[x, z] = (hv - center_shift * mid) / half_width
        return carry

    lax.fori_loop(0, planes - reach, body, 0)


def second_half_kernel(side_ref, rim_ref, a_ref, b_ref, psi_ref, pot_ref, out_ref, ext_ref):
    planes = psi_ref.shape[0]
    half = planes - reach
    depth, ny = out_ref.shape[1], out_ref.shape[3]
    h = side_ref[0]
    a_side = side_ref[1]
    ext_ref[pl.ds(reach + a_side * half, half)] = a_ref[...]
    ext_ref[pl.ds(reach + (1 - a_side) * half, half)] = b_ref[...]
    ext_ref[pl.ds(h * (reach + planes), reach)] = rim_ref[...]
    base = h * half

    def body(x, carry):
        for z in range(depth):
            hv, mid = ham_planes(ext_ref, pot_ref, base + x, z, ny)
            second = 2.0 / half_width * (hv - center_shift * mid) - psi_ref[base + x, z]
            out_ref[x, z] = second.astype(out_ref.dtype)
        return carry

    lax.fori_loop(0, half, body, 0)


def smem():
    return pl.BlockSpec(memory_space=pltpu.SMEM)


def whole(shape):
    return pl.BlockSpec(shape, lambda i: (0,) * len(shape))


def run_first_half(side, rim, mid, pot):
    planes, depth, states, ny = mid.shape
    half = (planes - reach, depth, states, ny)
    return pl.pallas_call(
        first_half_kernel,
        grid=(1,),
        in_specs=[smem(), whole(rim.shape), whole(mid.shape), whole(pot.shape)],
        out_specs=whole(half),
        out_shape=jax.ShapeDtypeStruct(half, jnp.float32),
        scratch_shapes=[pltpu.VMEM((planes + 2 * reach, depth, states, ny), jnp.float32)],
    )(side, rim, mid, pot)


def run_second_half(side, rim, a, b, psi, pot):
    planes, depth, states, ny = psi.shape
    return pl.pallas_call(
        second_half_kernel,
        grid=(1,),
        in_specs=[smem(), whole(rim.shape), whole(a.shape), whole(b.shape), whole(psi.shape), whole(pot.shape)],
        out_specs=whole(a.shape),
        out_shape=jax.ShapeDtypeStruct(a.shape, jnp.bfloat16),
        scratch_shapes=[pltpu.VMEM((planes + 2 * reach, depth, states, ny), jnp.float32)],
    )(side, rim, a, b, psi, pot)


def inner_outer(send_inner, send_outer):
    count = lax.axis_size("dom")
    inner = [(i, i + 1) if i % 2 == 0 else (i, i - 1) for i in range(count)]
    outer = [(i, (i - 1) % count) if i % 2 == 0 else (i, (i + 1) % count) for i in range(count)]
    return lax.ppermute(send_inner, "dom", inner), lax.ppermute(send_outer, "dom", outer)


def per_device(psi, potential, rotation):
    own_states, planes, depth, ny = psi.shape
    psi_t = psi.transpose(1, 2, 0, 3)
    pot_t = potential[:, :, None, :]
    if lax.axis_size("dom") % 2 or planes != 2 * reach:
        left, right = swap_rims(psi_t[:reach], psi_t[planes - reach :])
        first, head, tail = run_first(left, psi_t, right, pot_t)
        left, right = swap_rims(head, tail)
        second = run_second(left, first, right, psi_t, pot_t)
    else:
        even = lax.axis_index("dom") % 2 == 0
        hi = jnp.where(even, 1, 0).astype(jnp.int32)
        head, tail = psi_t[:reach], psi_t[planes - reach :]
        rim_in, rim_out = inner_outer(jnp.where(even, tail, head), jnp.where(even, head, tail))
        part_a = run_first_half(hi.reshape(1), rim_in, psi_t, pot_t)
        part_b = run_first_half((1 - hi).reshape(1), rim_out, psi_t, pot_t)
        rim_in, rim_out = inner_outer(part_a, part_b)
        sides_a = jnp.stack([hi, hi])
        sides_b = jnp.stack([1 - hi, hi])
        second_a = run_second_half(sides_a, rim_in, part_a, part_b, psi_t, pot_t)
        second_b = run_second_half(sides_b, rim_out, part_a, part_b, psi_t, pot_t)
        second = jnp.where(
            even,
            jnp.concatenate([second_b, second_a], axis=0),
            jnp.concatenate([second_a, second_b], axis=0),
        )
    filtered = second.astype(jnp.bfloat16).transpose(2, 0, 1, 3)
    rows = planes * depth
    count = lax.axis_size("band")
    chunk = rows * ny // count
    blocks = filtered.reshape(own_states, count, chunk).transpose(1, 0, 2)
    wire = (count, own_states * chunk // ny, ny)
    gathered = lax.all_to_all(blocks.reshape(wire), "band", 0, 0, tiled=True)
    mixed = lax.dot_general(
        rotation,
        gathered.reshape(own_states * count, chunk),
        (((0,), (0,)), ((), ())),
        preferred_element_type=jnp.float32,
    ).astype(jnp.bfloat16)
    back = lax.all_to_all(mixed.reshape(wire), "band", 0, 0, tiled=True)
    result = back.reshape(count, own_states, chunk).transpose(1, 0, 2)
    return result.reshape(psi.shape)


def solution(mesh):
    in_specs = (P("band", "dom", None, None), P("dom", None, None), P())
    out_specs = P("band", "dom", None, None)
    return jax.shard_map(
        per_device, mesh=mesh, in_specs=in_specs, out_specs=out_specs, check_vma=False
    )
```

```python
import jax
import jax.numpy as jnp
from jax import lax
from jax.experimental import pallas as pl
from jax.experimental.pallas import tpu as pltpu
from jax.sharding import PartitionSpec as P

coeffs = (
    -5369.0 / 1800.0,
    12.0 / 7.0,
    -15.0 / 56.0,
    10.0 / 189.0,
    -1.0 / 112.0,
    2.0 / 1925.0,
    -1.0 / 16632.0,
)
center_shift = 32.5
half_width = 27.5
reach = 6
state_block = 32


def swap_rims(head, tail):
    count = lax.axis_size("dom")
    if count % 2:
        left = lax.ppermute(tail, "dom", [(i, (i + 1) % count) for i in range(count)])
        right = lax.ppermute(head, "dom", [((i + 1) % count, i) for i in range(count)])
        return left, right
    even = lax.axis_index("dom") % 2 == 0
    inner = [(i, i + 1) if i % 2 == 0 else (i, i - 1) for i in range(count)]
    outer = [(i, (i - 1) % count) if i % 2 == 0 else (i, (i + 1) % count) for i in range(count)]
    got_inner = lax.ppermute(jnp.where(even, tail, head), "dom", inner)
    got_outer = lax.ppermute(jnp.where(even, head, tail), "dom", outer)
    left = jnp.where(even, got_outer, got_inner)
    right = jnp.where(even, got_inner, got_outer)
    return left, right


def ham_planes(ext_ref, pot_ref, x, z, ny):
    mid = ext_ref[x + reach, z]
    lap = (3.0 * coeffs[0]) * mid
    for k in range(1, 7):
        lap = lap + coeffs[k] * (ext_ref[x + reach + k, z] + ext_ref[x + reach - k, z])
    for k in range(1, 7):
        lap = lap + coeffs[k] * (pltpu.roll(mid, k, 1) + pltpu.roll(mid, ny - k, 1))
    lap = lap + coeffs[1] * ext_ref[x + reach, 1 - z]
    return -2.0 * lap + pot_ref[x, z] * mid, mid


def fill_ext(left_ref, mid_ref, right_ref, ext_ref):
    planes = mid_ref.shape[0]
    ext_ref[pl.ds(0, reach)] = left_ref[...]
    ext_ref[pl.ds(reach, planes)] = mid_ref[...]
    ext_ref[pl.ds(reach + planes, reach)] = right_ref[...]


def first_kernel(left_ref, mid_ref, right_ref, pot_ref, out_ref, head_ref, tail_ref, ext_ref):
    planes, depth, _, ny = out_ref.shape
    fill_ext(left_ref, mid_ref, right_ref, ext_ref)

    def body(x, carry):
        for z in range(depth):
            h, mid = ham_planes(ext_ref, pot_ref, x, z, ny)
            out_ref[x, z] = (h - center_shift * mid) / half_width
        return carry

    lax.fori_loop(0, planes, body, 0)
    head_ref[...] = out_ref[pl.ds(0, reach)]
    tail_ref[...] = out_ref[pl.ds(planes - reach, reach)]


def second_kernel(left_ref, mid_ref, right_ref, psi_ref, pot_ref, out_ref, ext_ref):
    planes, depth, _, ny = out_ref.shape
    fill_ext(left_ref, mid_ref, right_ref, ext_ref)

    def body(x, carry):
        for z in range(depth):
            h, mid = ham_planes(ext_ref, pot_ref, x, z, ny)
            out_ref[x, z] = 2.0 / half_width * (h - center_shift * mid) - psi_ref[x, z]
        return carry

    lax.fori_loop(0, planes, body, 0)


def specs(mid, sb):
    planes, depth, _, ny = mid.shape
    rim = pl.BlockSpec((reach, depth, sb, ny), lambda i: (0, 0, i, 0))
    body = pl.BlockSpec((planes, depth, sb, ny), lambda i: (0, 0, i, 0))
    pot = pl.BlockSpec((planes, depth, 1, ny), lambda i: (0, 0, 0, 0))
    ext = pltpu.VMEM((planes + 2 * reach, depth, sb, ny), jnp.float32)
    return rim, body, pot, ext


def run_first(left, mid, right, pot):
    sb = state_block
    rim, body, pot_spec, ext = specs(mid, sb)
    return pl.pallas_call(
        first_kernel,
        grid=(mid.shape[2] // sb,),
        in_specs=[rim, body, rim, pot_spec],
        out_specs=[body, rim, rim],
        out_shape=[
            jax.ShapeDtypeStruct(mid.shape, jnp.float32),
            jax.ShapeDtypeStruct(left.shape, jnp.float32),
            jax.ShapeDtypeStruct(left.shape, jnp.float32),
        ],
        scratch_shapes=[ext],
    )(left, mid, right, pot)


def run_second(left, mid, right, psi, pot):
    sb = state_block
    rim, body, pot_spec, ext = specs(mid, sb)
    return pl.pallas_call(
        second_kernel,
        grid=(mid.shape[2] // sb,),
        in_specs=[rim, body, rim, body, pot_spec],
        out_specs=body,
        out_shape=jax.ShapeDtypeStruct(mid.shape, jnp.float32),
        scratch_shapes=[ext],
    )(left, mid, right, psi, pot)


def first_half_kernel(side_ref, rim_ref, mid_ref, pot_ref, out_ref, ext_ref):
    planes = mid_ref.shape[0]
    depth, ny = out_ref.shape[1], out_ref.shape[3]
    h = side_ref[0]
    ext_ref[pl.ds(reach, planes)] = mid_ref[...]
    ext_ref[pl.ds(h * (reach + planes), reach)] = rim_ref[...]
    base = h * (planes - reach)

    def body(x, carry):
        for z in range(depth):
            hv, mid = ham_planes(ext_ref, pot_ref, base + x, z, ny)
            out_ref[x, z] = (hv - center_shift * mid) / half_width
        return carry

    lax.fori_loop(0, planes - reach, body, 0)


def second_half_kernel(side_ref, rim_ref, a_ref, b_ref, psi_ref, pot_ref, out_ref, ext_ref):
    planes = psi_ref.shape[0]
    half = planes - reach
    depth, ny = out_ref.shape[1], out_ref.shape[3]
    h = side_ref[0]
    a_side = side_ref[1]
    ext_ref[pl.ds(reach + a_side * half, half)] = a_ref[...]
    ext_ref[pl.ds(reach + (1 - a_side) * half, half)] = b_ref[...]
    ext_ref[pl.ds(h * (reach + planes), reach)] = rim_ref[...]
    base = h * half

    def body(x, carry):
        for z in range(depth):
            hv, mid = ham_planes(ext_ref, pot_ref, base + x, z, ny)
            out_ref[x, z] = 2.0 / half_width * (hv - center_shift * mid) - psi_ref[base + x, z]
        return carry

    lax.fori_loop(0, half, body, 0)


def smem():
    return pl.BlockSpec(memory_space=pltpu.SMEM)


def whole(shape):
    return pl.BlockSpec(shape, lambda i: (0,) * len(shape))


def run_first_half(side, rim, mid, pot):
    planes, depth, states, ny = mid.shape
    half = (planes - reach, depth, states, ny)
    return pl.pallas_call(
        first_half_kernel,
        grid=(1,),
        in_specs=[smem(), whole(rim.shape), whole(mid.shape), whole(pot.shape)],
        out_specs=whole(half),
        out_shape=jax.ShapeDtypeStruct(half, jnp.float32),
        scratch_shapes=[pltpu.VMEM((planes + 2 * reach, depth, states, ny), jnp.float32)],
    )(side, rim, mid, pot)


def run_second_half(side, rim, a, b, psi, pot):
    planes, depth, states, ny = psi.shape
    return pl.pallas_call(
        second_half_kernel,
        grid=(1,),
        in_specs=[smem(), whole(rim.shape), whole(a.shape), whole(b.shape), whole(psi.shape), whole(pot.shape)],
        out_specs=whole(a.shape),
        out_shape=jax.ShapeDtypeStruct(a.shape, jnp.float32),
        scratch_shapes=[pltpu.VMEM((planes + 2 * reach, depth, states, ny), jnp.float32)],
    )(side, rim, a, b, psi, pot)


def inner_outer(send_inner, send_outer):
    count = lax.axis_size("dom")
    inner = [(i, i + 1) if i % 2 == 0 else (i, i - 1) for i in range(count)]
    outer = [(i, (i - 1) % count) if i % 2 == 0 else (i, (i + 1) % count) for i in range(count)]
    return lax.ppermute(send_inner, "dom", inner), lax.ppermute(send_outer, "dom", outer)


def to_wire(second, parts):
    planes, depth, states, ny = second.shape
    chunk = planes * depth * ny // parts
    flat = second.astype(jnp.bfloat16).transpose(2, 0, 1, 3).reshape(states, parts, chunk)
    return flat.transpose(1, 0, 2).reshape(parts, states * chunk // ny, ny)


def per_device(psi, potential, rotation):
    own_states, planes, depth, ny = psi.shape
    psi_t = psi.transpose(1, 2, 0, 3)
    pot_t = potential[:, :, None, :]
    rows = planes * depth
    count = lax.axis_size("band")
    chunk = rows * ny // count
    wire = (count, own_states * chunk // ny, ny)
    if lax.axis_size("dom") % 2 or planes != 2 * reach or count % 2:
        left, right = swap_rims(psi_t[:reach], psi_t[planes - reach :])
        first, head, tail = run_first(left, psi_t, right, pot_t)
        left, right = swap_rims(head, tail)
        second = run_second(left, first, right, psi_t, pot_t)
        blocks = to_wire(second, count)
    else:
        even = lax.axis_index("dom") % 2 == 0
        hi = jnp.where(even, 1, 0).astype(jnp.int32)
        head, tail = psi_t[:reach], psi_t[planes - reach :]
        rim_in, rim_out = inner_outer(jnp.where(even, tail, head), jnp.where(even, head, tail))
        part_a = run_first_half(hi.reshape(1), rim_in, psi_t, pot_t)
        part_b = run_first_half((1 - hi).reshape(1), rim_out, psi_t, pot_t)
        rim_in, rim_out = inner_outer(part_a, part_b)
        sides_a = jnp.stack([hi, hi])
        sides_b = jnp.stack([1 - hi, hi])
        second_a = run_second_half(sides_a, rim_in, part_a, part_b, psi_t, pot_t)
        second_b = run_second_half(sides_b, rim_out, part_a, part_b, psi_t, pot_t)
        wire_a = to_wire(second_a, count // 2)
        wire_b = to_wire(second_b, count // 2)
        blocks = jnp.where(
            even,
            jnp.concatenate([wire_b, wire_a], axis=0),
            jnp.concatenate([wire_a, wire_b], axis=0),
        )
    gathered = lax.all_to_all(blocks, "band", 0, 0, tiled=True)
    mixed = lax.dot_general(
        rotation,
        gathered.reshape(own_states * count, chunk),
        (((0,), (0,)), ((), ())),
        preferred_element_type=jnp.float32,
    ).astype(jnp.bfloat16)
    back = lax.all_to_all(mixed.reshape(wire), "band", 0, 0, tiled=True)
    result = back.reshape(count, own_states, chunk).transpose(1, 0, 2)
    return result.reshape(psi.shape)


def solution(mesh):
    in_specs = (P("band", "dom", None, None), P("dom", None, None), P())
    out_specs = P("band", "dom", None, None)
    return jax.shard_map(
        per_device, mesh=mesh, in_specs=in_specs, out_specs=out_specs, check_vma=False
    )
```

```python
import jax
import jax.numpy as jnp
from jax import lax
from jax.experimental import pallas as pl
from jax.experimental.pallas import tpu as pltpu
from jax.sharding import PartitionSpec as P

coeffs = (
    -5369.0 / 1800.0,
    12.0 / 7.0,
    -15.0 / 56.0,
    10.0 / 189.0,
    -1.0 / 112.0,
    2.0 / 1925.0,
    -1.0 / 16632.0,
)
center_shift = 32.5
half_width = 27.5
reach = 6
state_block = 32


def swap_rims(head, tail):
    count = lax.axis_size("dom")
    if count % 2:
        left = lax.ppermute(tail, "dom", [(i, (i + 1) % count) for i in range(count)])
        right = lax.ppermute(head, "dom", [((i + 1) % count, i) for i in range(count)])
        return left, right
    even = lax.axis_index("dom") % 2 == 0
    inner = [(i, i + 1) if i % 2 == 0 else (i, i - 1) for i in range(count)]
    outer = [(i, (i - 1) % count) if i % 2 == 0 else (i, (i + 1) % count) for i in range(count)]
    got_inner = lax.ppermute(jnp.where(even, tail, head), "dom", inner)
    got_outer = lax.ppermute(jnp.where(even, head, tail), "dom", outer)
    left = jnp.where(even, got_outer, got_inner)
    right = jnp.where(even, got_inner, got_outer)
    return left, right


def ham_planes(ext_ref, pot_ref, x, z, ny):
    mid = ext_ref[x + reach, z]
    lap = (3.0 * coeffs[0]) * mid
    for k in range(1, 7):
        lap = lap + coeffs[k] * (ext_ref[x + reach + k, z] + ext_ref[x + reach - k, z])
    for k in range(1, 7):
        lap = lap + coeffs[k] * (pltpu.roll(mid, k, 1) + pltpu.roll(mid, ny - k, 1))
    lap = lap + coeffs[1] * ext_ref[x + reach, 1 - z]
    return -2.0 * lap + pot_ref[x, z] * mid, mid


def fill_ext(left_ref, mid_ref, right_ref, ext_ref):
    planes = mid_ref.shape[0]
    ext_ref[pl.ds(0, reach)] = left_ref[...]
    ext_ref[pl.ds(reach, planes)] = mid_ref[...]
    ext_ref[pl.ds(reach + planes, reach)] = right_ref[...]


def first_kernel(left_ref, mid_ref, right_ref, pot_ref, out_ref, head_ref, tail_ref, ext_ref):
    planes, depth, _, ny = out_ref.shape
    fill_ext(left_ref, mid_ref, right_ref, ext_ref)

    def body(x, carry):
        for z in range(depth):
            h, mid = ham_planes(ext_ref, pot_ref, x, z, ny)
            out_ref[x, z] = (h - center_shift * mid) / half_width
        return carry

    lax.fori_loop(0, planes, body, 0)
    head_ref[...] = out_ref[pl.ds(0, reach)]
    tail_ref[...] = out_ref[pl.ds(planes - reach, reach)]


def second_kernel(left_ref, mid_ref, right_ref, psi_ref, pot_ref, out_ref, ext_ref):
    planes, depth, _, ny = out_ref.shape
    fill_ext(left_ref, mid_ref, right_ref, ext_ref)

    def body(x, carry):
        for z in range(depth):
            h, mid = ham_planes(ext_ref, pot_ref, x, z, ny)
            out_ref[x, z] = 2.0 / half_width * (h - center_shift * mid) - psi_ref[x, z]
        return carry

    lax.fori_loop(0, planes, body, 0)


def specs(mid, sb):
    planes, depth, _, ny = mid.shape
    rim = pl.BlockSpec((reach, depth, sb, ny), lambda i: (0, 0, i, 0))
    body = pl.BlockSpec((planes, depth, sb, ny), lambda i: (0, 0, i, 0))
    pot = pl.BlockSpec((planes, depth, 1, ny), lambda i: (0, 0, 0, 0))
    ext = pltpu.VMEM((planes + 2 * reach, depth, sb, ny), jnp.float32)
    return rim, body, pot, ext


def run_first(left, mid, right, pot):
    sb = state_block
    rim, body, pot_spec, ext = specs(mid, sb)
    return pl.pallas_call(
        first_kernel,
        grid=(mid.shape[2] // sb,),
        in_specs=[rim, body, rim, pot_spec],
        out_specs=[body, rim, rim],
        out_shape=[
            jax.ShapeDtypeStruct(mid.shape, jnp.float32),
            jax.ShapeDtypeStruct(left.shape, jnp.float32),
            jax.ShapeDtypeStruct(left.shape, jnp.float32),
        ],
        scratch_shapes=[ext],
    )(left, mid, right, pot)


def run_second(left, mid, right, psi, pot):
    sb = state_block
    rim, body, pot_spec, ext = specs(mid, sb)
    return pl.pallas_call(
        second_kernel,
        grid=(mid.shape[2] // sb,),
        in_specs=[rim, body, rim, body, pot_spec],
        out_specs=body,
        out_shape=jax.ShapeDtypeStruct(mid.shape, jnp.float32),
        scratch_shapes=[ext],
    )(left, mid, right, psi, pot)


def first_half_kernel(side_ref, rim_ref, mid_ref, pot_ref, out_ref, ext_ref):
    planes = mid_ref.shape[0]
    depth, ny = out_ref.shape[1], out_ref.shape[3]
    h = side_ref[0]
    ext_ref[pl.ds(reach, planes)] = mid_ref[...]
    ext_ref[pl.ds(h * (reach + planes), reach)] = rim_ref[...]
    base = h * (planes - reach)

    def body(x, carry):
        for z in range(depth):
            hv, mid = ham_planes(ext_ref, pot_ref, base + x, z, ny)
            out_ref[x, z] = (hv - center_shift * mid) / half_width
        return carry

    lax.fori_loop(0, planes - reach, body, 0)


def second_half_kernel(side_ref, rim_ref, a_ref, b_ref, psi_ref, pot_ref, out_ref, ext_ref):
    planes = psi_ref.shape[0]
    half = planes - reach
    depth, ny = out_ref.shape[1], out_ref.shape[3]
    h = side_ref[0]
    a_side = side_ref[1]
    ext_ref[pl.ds(reach + a_side * half, half)] = a_ref[...]
    ext_ref[pl.ds(reach + (1 - a_side) * half, half)] = b_ref[...]
    ext_ref[pl.ds(h * (reach + planes), reach)] = rim_ref[...]
    base = h * half

    def body(x, carry):
        for z in range(depth):
            hv, mid = ham_planes(ext_ref, pot_ref, base + x, z, ny)
            out_ref[x, z] = 2.0 / half_width * (hv - center_shift * mid) - psi_ref[base + x, z]
        return carry

    lax.fori_loop(0, half, body, 0)


def smem():
    return pl.BlockSpec(memory_space=pltpu.SMEM)


def whole(shape):
    return pl.BlockSpec(shape, lambda i: (0,) * len(shape))


def run_first_half(side, rim, mid, pot):
    planes, depth, states, ny = mid.shape
    half = (planes - reach, depth, states, ny)
    return pl.pallas_call(
        first_half_kernel,
        grid=(1,),
        in_specs=[smem(), whole(rim.shape), whole(mid.shape), whole(pot.shape)],
        out_specs=whole(half),
        out_shape=jax.ShapeDtypeStruct(half, jnp.float32),
        scratch_shapes=[pltpu.VMEM((planes + 2 * reach, depth, states, ny), jnp.float32)],
    )(side, rim, mid, pot)


def run_second_half(side, rim, a, b, psi, pot):
    planes, depth, states, ny = psi.shape
    return pl.pallas_call(
        second_half_kernel,
        grid=(1,),
        in_specs=[smem(), whole(rim.shape), whole(a.shape), whole(b.shape), whole(psi.shape), whole(pot.shape)],
        out_specs=whole(a.shape),
        out_shape=jax.ShapeDtypeStruct(a.shape, jnp.float32),
        scratch_shapes=[pltpu.VMEM((planes + 2 * reach, depth, states, ny), jnp.float32)],
    )(side, rim, a, b, psi, pot)


def inner_outer(send_inner, send_outer):
    count = lax.axis_size("dom")
    inner = [(i, i + 1) if i % 2 == 0 else (i, i - 1) for i in range(count)]
    outer = [(i, (i - 1) % count) if i % 2 == 0 else (i, (i + 1) % count) for i in range(count)]
    return lax.ppermute(send_inner, "dom", inner), lax.ppermute(send_outer, "dom", outer)


def to_wire(second, parts):
    planes, depth, states, ny = second.shape
    chunk = planes * depth * ny // parts
    flat = second.astype(jnp.bfloat16).transpose(2, 0, 1, 3).reshape(states, parts, chunk)
    return flat.transpose(1, 0, 2).reshape(parts, states * chunk // ny, ny)


def per_device(psi, potential, rotation):
    own_states, planes, depth, ny = psi.shape
    psi_t = psi.transpose(1, 2, 0, 3)
    pot_t = potential[:, :, None, :]
    rows = planes * depth
    count = lax.axis_size("band")
    chunk = rows * ny // count
    wire = (count, own_states * chunk // ny, ny)
    if lax.axis_size("dom") % 2 or planes != 2 * reach or count % 2:
        left, right = swap_rims(psi_t[:reach], psi_t[planes - reach :])
        first, head, tail = run_first(left, psi_t, right, pot_t)
        left, right = swap_rims(head, tail)
        second = run_second(left, first, right, psi_t, pot_t)
        blocks = to_wire(second, count)
    else:
        even = lax.axis_index("dom") % 2 == 0
        hi = jnp.where(even, 1, 0).astype(jnp.int32)
        head, tail = psi_t[:reach], psi_t[planes - reach :]
        rim_in, rim_out = inner_outer(jnp.where(even, tail, head), jnp.where(even, head, tail))
        part_a = run_first_half(hi.reshape(1), rim_in, psi_t, pot_t)
        _, rim_out = lax.optimization_barrier((part_a, rim_out))
        part_b = run_first_half((1 - hi).reshape(1), rim_out, psi_t, pot_t)
        rim_in, rim_out = inner_outer(part_a, part_b)
        sides_a = jnp.stack([hi, hi])
        sides_b = jnp.stack([1 - hi, hi])
        second_a = run_second_half(sides_a, rim_in, part_a, part_b, psi_t, pot_t)
        _, rim_out = lax.optimization_barrier((second_a, rim_out))
        second_b = run_second_half(sides_b, rim_out, part_a, part_b, psi_t, pot_t)
        wire_a = to_wire(second_a, count // 2)
        wire_b = to_wire(second_b, count // 2)
        blocks = jnp.where(
            even,
            jnp.concatenate([wire_b, wire_a], axis=0),
            jnp.concatenate([wire_a, wire_b], axis=0),
        )
    gathered = lax.all_to_all(blocks, "band", 0, 0, tiled=True)
    mixed = lax.dot_general(
        rotation,
        gathered.reshape(own_states * count, chunk),
        (((0,), (0,)), ((), ())),
        preferred_element_type=jnp.float32,
    ).astype(jnp.bfloat16)
    back = lax.all_to_all(mixed.reshape(wire), "band", 0, 0, tiled=True)
    result = back.reshape(count, own_states, chunk).transpose(1, 0, 2)
    return result.reshape(psi.shape)


def solution(mesh):
    in_specs = (P("band", "dom", None, None), P("dom", None, None), P())
    out_specs = P("band", "dom", None, None)
    return jax.shard_map(
        per_device, mesh=mesh, in_specs=in_specs, out_specs=out_specs, check_vma=False
    )
```

```python
import jax
import jax.numpy as jnp
from jax import lax
from jax.experimental import pallas as pl
from jax.experimental.pallas import tpu as pltpu
from jax.sharding import PartitionSpec as P

coeffs = (
    -5369.0 / 1800.0,
    12.0 / 7.0,
    -15.0 / 56.0,
    10.0 / 189.0,
    -1.0 / 112.0,
    2.0 / 1925.0,
    -1.0 / 16632.0,
)
center_shift = 32.5
half_width = 27.5
reach = 6
state_block = 32


def swap_rims(head, tail):
    count = lax.axis_size("dom")
    if count % 2:
        left = lax.ppermute(tail, "dom", [(i, (i + 1) % count) for i in range(count)])
        right = lax.ppermute(head, "dom", [((i + 1) % count, i) for i in range(count)])
        return left, right
    even = lax.axis_index("dom") % 2 == 0
    inner = [(i, i + 1) if i % 2 == 0 else (i, i - 1) for i in range(count)]
    outer = [(i, (i - 1) % count) if i % 2 == 0 else (i, (i + 1) % count) for i in range(count)]
    got_inner = lax.ppermute(jnp.where(even, tail, head), "dom", inner)
    got_outer = lax.ppermute(jnp.where(even, head, tail), "dom", outer)
    left = jnp.where(even, got_outer, got_inner)
    right = jnp.where(even, got_inner, got_outer)
    return left, right


def ham_planes(ext_ref, pot_ref, x, z, ny):
    mid = ext_ref[x + reach, z]
    lap = (3.0 * coeffs[0]) * mid
    for k in range(1, 7):
        lap = lap + coeffs[k] * (ext_ref[x + reach + k, z] + ext_ref[x + reach - k, z])
    for k in range(1, 7):
        lap = lap + coeffs[k] * (pltpu.roll(mid, k, 1) + pltpu.roll(mid, ny - k, 1))
    lap = lap + coeffs[1] * ext_ref[x + reach, 1 - z]
    return -2.0 * lap + pot_ref[x, z] * mid, mid


def fill_ext(left_ref, mid_ref, right_ref, ext_ref):
    planes = mid_ref.shape[0]
    ext_ref[pl.ds(0, reach)] = left_ref[...]
    ext_ref[pl.ds(reach, planes)] = mid_ref[...]
    ext_ref[pl.ds(reach + planes, reach)] = right_ref[...]


def first_kernel(left_ref, mid_ref, right_ref, pot_ref, out_ref, head_ref, tail_ref, ext_ref):
    planes, depth, _, ny = out_ref.shape
    fill_ext(left_ref, mid_ref, right_ref, ext_ref)

    def body(x, carry):
        for z in range(depth):
            h, mid = ham_planes(ext_ref, pot_ref, x, z, ny)
            out_ref[x, z] = (h - center_shift * mid) / half_width
        return carry

    lax.fori_loop(0, planes, body, 0)
    head_ref[...] = out_ref[pl.ds(0, reach)]
    tail_ref[...] = out_ref[pl.ds(planes - reach, reach)]


def second_kernel(left_ref, mid_ref, right_ref, psi_ref, pot_ref, out_ref, ext_ref):
    planes, depth, _, ny = out_ref.shape
    fill_ext(left_ref, mid_ref, right_ref, ext_ref)

    def body(x, carry):
        for z in range(depth):
            h, mid = ham_planes(ext_ref, pot_ref, x, z, ny)
            out_ref[x, z] = 2.0 / half_width * (h - center_shift * mid) - psi_ref[x, z]
        return carry

    lax.fori_loop(0, planes, body, 0)


def specs(mid, sb):
    planes, depth, _, ny = mid.shape
    rim = pl.BlockSpec((reach, depth, sb, ny), lambda i: (0, 0, i, 0))
    body = pl.BlockSpec((planes, depth, sb, ny), lambda i: (0, 0, i, 0))
    pot = pl.BlockSpec((planes, depth, 1, ny), lambda i: (0, 0, 0, 0))
    ext = pltpu.VMEM((planes + 2 * reach, depth, sb, ny), jnp.float32)
    return rim, body, pot, ext


def run_first(left, mid, right, pot):
    sb = state_block
    rim, body, pot_spec, ext = specs(mid, sb)
    return pl.pallas_call(
        first_kernel,
        grid=(mid.shape[2] // sb,),
        in_specs=[rim, body, rim, pot_spec],
        out_specs=[body, rim, rim],
        out_shape=[
            jax.ShapeDtypeStruct(mid.shape, jnp.float32),
            jax.ShapeDtypeStruct(left.shape, jnp.float32),
            jax.ShapeDtypeStruct(left.shape, jnp.float32),
        ],
        scratch_shapes=[ext],
    )(left, mid, right, pot)


def run_second(left, mid, right, psi, pot):
    sb = state_block
    rim, body, pot_spec, ext = specs(mid, sb)
    return pl.pallas_call(
        second_kernel,
        grid=(mid.shape[2] // sb,),
        in_specs=[rim, body, rim, body, pot_spec],
        out_specs=body,
        out_shape=jax.ShapeDtypeStruct(mid.shape, jnp.float32),
        scratch_shapes=[ext],
    )(left, mid, right, psi, pot)


def first_half_kernel(side_ref, rim_ref, mid_ref, pot_ref, out_ref, ext_ref):
    planes = mid_ref.shape[0]
    depth, ny = out_ref.shape[1], out_ref.shape[3]
    h = side_ref[0]
    ext_ref[pl.ds(reach, planes)] = mid_ref[...]
    ext_ref[pl.ds(h * (reach + planes), reach)] = rim_ref[...]
    base = h * (planes - reach)

    def body(x, carry):
        for z in range(depth):
            hv, mid = ham_planes(ext_ref, pot_ref, base + x, z, ny)
            out_ref[x, z] = (hv - center_shift * mid) / half_width
        return carry

    lax.fori_loop(0, planes - reach, body, 0)


def second_half_kernel(side_ref, rim_ref, a_ref, b_ref, psi_ref, pot_ref, out_ref, ext_ref):
    planes = psi_ref.shape[0]
    half = planes - reach
    depth, ny = out_ref.shape[1], out_ref.shape[3]
    h = side_ref[0]
    a_side = side_ref[1]
    ext_ref[pl.ds(reach + a_side * half, half)] = a_ref[...]
    ext_ref[pl.ds(reach + (1 - a_side) * half, half)] = b_ref[...]
    ext_ref[pl.ds(h * (reach + planes), reach)] = rim_ref[...]
    base = h * half

    def body(x, carry):
        for z in range(depth):
            hv, mid = ham_planes(ext_ref, pot_ref, base + x, z, ny)
            second = 2.0 / half_width * (hv - center_shift * mid) - psi_ref[base + x, z]
            out_ref[x, z] = second.astype(out_ref.dtype)
        return carry

    lax.fori_loop(0, half, body, 0)


def smem():
    return pl.BlockSpec(memory_space=pltpu.SMEM)


def whole(shape):
    return pl.BlockSpec(shape, lambda i: (0,) * len(shape))


def run_first_half(side, rim, mid, pot):
    planes, depth, states, ny = mid.shape
    half = (planes - reach, depth, states, ny)
    return pl.pallas_call(
        first_half_kernel,
        grid=(1,),
        in_specs=[smem(), whole(rim.shape), whole(mid.shape), whole(pot.shape)],
        out_specs=whole(half),
        out_shape=jax.ShapeDtypeStruct(half, jnp.float32),
        scratch_shapes=[pltpu.VMEM((planes + 2 * reach, depth, states, ny), jnp.float32)],
    )(side, rim, mid, pot)


def run_second_half(side, rim, a, b, psi, pot):
    planes, depth, states, ny = psi.shape
    return pl.pallas_call(
        second_half_kernel,
        grid=(1,),
        in_specs=[smem(), whole(rim.shape), whole(a.shape), whole(b.shape), whole(psi.shape), whole(pot.shape)],
        out_specs=whole(a.shape),
        out_shape=jax.ShapeDtypeStruct(a.shape, jnp.bfloat16),
        scratch_shapes=[pltpu.VMEM((planes + 2 * reach, depth, states, ny), jnp.float32)],
    )(side, rim, a, b, psi, pot)


def inner_outer(send_inner, send_outer):
    count = lax.axis_size("dom")
    inner = [(i, i + 1) if i % 2 == 0 else (i, i - 1) for i in range(count)]
    outer = [(i, (i - 1) % count) if i % 2 == 0 else (i, (i + 1) % count) for i in range(count)]
    return lax.ppermute(send_inner, "dom", inner), lax.ppermute(send_outer, "dom", outer)


def to_wire(second, parts):
    planes, depth, states, ny = second.shape
    chunk = planes * depth * ny // parts
    flat = second.astype(jnp.bfloat16).transpose(2, 0, 1, 3).reshape(states, parts, chunk)
    return flat.transpose(1, 0, 2).reshape(parts, states * chunk // ny, ny)


def per_device(psi, potential, rotation):
    own_states, planes, depth, ny = psi.shape
    psi_t = psi.transpose(1, 2, 0, 3)
    pot_t = potential[:, :, None, :]
    rows = planes * depth
    count = lax.axis_size("band")
    chunk = rows * ny // count
    wire = (count, own_states * chunk // ny, ny)
    if lax.axis_size("dom") % 2 or planes != 2 * reach or count % 2:
        left, right = swap_rims(psi_t[:reach], psi_t[planes - reach :])
        first, head, tail = run_first(left, psi_t, right, pot_t)
        left, right = swap_rims(head, tail)
        second = run_second(left, first, right, psi_t, pot_t)
        blocks = to_wire(second, count)
    else:
        even = lax.axis_index("dom") % 2 == 0
        hi = jnp.where(even, 1, 0).astype(jnp.int32)
        head, tail = psi_t[:reach], psi_t[planes - reach :]
        rim_in, rim_out = inner_outer(jnp.where(even, tail, head), jnp.where(even, head, tail))
        part_a = run_first_half(hi.reshape(1), rim_in, psi_t, pot_t)
        _, rim_out = lax.optimization_barrier((part_a, rim_out))
        part_b = run_first_half((1 - hi).reshape(1), rim_out, psi_t, pot_t)
        rim_in, rim_out = inner_outer(part_a, part_b)
        sides_a = jnp.stack([hi, hi])
        sides_b = jnp.stack([1 - hi, hi])
        second_a = run_second_half(sides_a, rim_in, part_a, part_b, psi_t, pot_t)
        _, rim_out = lax.optimization_barrier((second_a, rim_out))
        second_b = run_second_half(sides_b, rim_out, part_a, part_b, psi_t, pot_t)
        wire_a = to_wire(second_a, count // 2)
        wire_b = to_wire(second_b, count // 2)
        blocks = jnp.where(
            even,
            jnp.concatenate([wire_b, wire_a], axis=0),
            jnp.concatenate([wire_a, wire_b], axis=0),
        )
    gathered = lax.all_to_all(blocks, "band", 0, 0, tiled=True)
    mixed = lax.dot_general(
        rotation,
        gathered.reshape(own_states * count, chunk),
        (((0,), (0,)), ((), ())),
        preferred_element_type=jnp.float32,
    ).astype(jnp.bfloat16)
    back = lax.all_to_all(mixed.reshape(wire), "band", 0, 0, tiled=True)
    result = back.reshape(count, own_states, chunk).transpose(1, 0, 2)
    return result.reshape(psi.shape)


def solution(mesh):
    in_specs = (P("band", "dom", None, None), P("dom", None, None), P())
    out_specs = P("band", "dom", None, None)
    return jax.shard_map(
        per_device, mesh=mesh, in_specs=in_specs, out_specs=out_specs, check_vma=False
    )
```

```python
import jax
import jax.numpy as jnp
from jax import lax
from jax.experimental import pallas as pl
from jax.experimental.pallas import tpu as pltpu
from jax.sharding import PartitionSpec as P

coeffs = (
    -5369.0 / 1800.0,
    12.0 / 7.0,
    -15.0 / 56.0,
    10.0 / 189.0,
    -1.0 / 112.0,
    2.0 / 1925.0,
    -1.0 / 16632.0,
)
center_shift = 32.5
half_width = 27.5
reach = 6
state_block = 32


def swap_rims(head, tail):
    count = lax.axis_size("dom")
    if count % 2:
        left = lax.ppermute(tail, "dom", [(i, (i + 1) % count) for i in range(count)])
        right = lax.ppermute(head, "dom", [((i + 1) % count, i) for i in range(count)])
        return left, right
    even = lax.axis_index("dom") % 2 == 0
    inner = [(i, i + 1) if i % 2 == 0 else (i, i - 1) for i in range(count)]
    outer = [(i, (i - 1) % count) if i % 2 == 0 else (i, (i + 1) % count) for i in range(count)]
    got_inner = lax.ppermute(jnp.where(even, tail, head), "dom", inner)
    got_outer = lax.ppermute(jnp.where(even, head, tail), "dom", outer)
    left = jnp.where(even, got_outer, got_inner)
    right = jnp.where(even, got_inner, got_outer)
    return left, right


def ham_planes(ext_ref, pot_ref, x, z, ny):
    mid = ext_ref[x + reach, z]
    lap = (3.0 * coeffs[0]) * mid
    for k in range(1, 7):
        lap = lap + coeffs[k] * (ext_ref[x + reach + k, z] + ext_ref[x + reach - k, z])
    for k in range(1, 7):
        lap = lap + coeffs[k] * (pltpu.roll(mid, k, 1) + pltpu.roll(mid, ny - k, 1))
    lap = lap + coeffs[1] * ext_ref[x + reach, 1 - z]
    return -2.0 * lap + pot_ref[x, z] * mid, mid


def fill_ext(left_ref, mid_ref, right_ref, ext_ref):
    planes = mid_ref.shape[0]
    ext_ref[pl.ds(0, reach)] = left_ref[...]
    ext_ref[pl.ds(reach, planes)] = mid_ref[...]
    ext_ref[pl.ds(reach + planes, reach)] = right_ref[...]


def first_kernel(left_ref, mid_ref, right_ref, pot_ref, out_ref, head_ref, tail_ref, ext_ref):
    planes, depth, _, ny = out_ref.shape
    fill_ext(left_ref, mid_ref, right_ref, ext_ref)

    def body(x, carry):
        for z in range(depth):
            h, mid = ham_planes(ext_ref, pot_ref, x, z, ny)
            out_ref[x, z] = (h - center_shift * mid) / half_width
        return carry

    lax.fori_loop(0, planes, body, 0)
    head_ref[...] = out_ref[pl.ds(0, reach)]
    tail_ref[...] = out_ref[pl.ds(planes - reach, reach)]


def second_kernel(left_ref, mid_ref, right_ref, psi_ref, pot_ref, out_ref, ext_ref):
    planes, depth, _, ny = out_ref.shape
    fill_ext(left_ref, mid_ref, right_ref, ext_ref)

    def body(x, carry):
        for z in range(depth):
            h, mid = ham_planes(ext_ref, pot_ref, x, z, ny)
            out_ref[x, z] = 2.0 / half_width * (h - center_shift * mid) - psi_ref[x, z]
        return carry

    lax.fori_loop(0, planes, body, 0)


def specs(mid, sb):
    planes, depth, _, ny = mid.shape
    rim = pl.BlockSpec((reach, depth, sb, ny), lambda i: (0, 0, i, 0))
    body = pl.BlockSpec((planes, depth, sb, ny), lambda i: (0, 0, i, 0))
    pot = pl.BlockSpec((planes, depth, 1, ny), lambda i: (0, 0, 0, 0))
    ext = pltpu.VMEM((planes + 2 * reach, depth, sb, ny), jnp.float32)
    return rim, body, pot, ext


def run_first(left, mid, right, pot):
    sb = state_block
    rim, body, pot_spec, ext = specs(mid, sb)
    return pl.pallas_call(
        first_kernel,
        grid=(mid.shape[2] // sb,),
        in_specs=[rim, body, rim, pot_spec],
        out_specs=[body, rim, rim],
        out_shape=[
            jax.ShapeDtypeStruct(mid.shape, jnp.float32),
            jax.ShapeDtypeStruct(left.shape, jnp.float32),
            jax.ShapeDtypeStruct(left.shape, jnp.float32),
        ],
        scratch_shapes=[ext],
    )(left, mid, right, pot)


def run_second(left, mid, right, psi, pot):
    sb = state_block
    rim, body, pot_spec, ext = specs(mid, sb)
    return pl.pallas_call(
        second_kernel,
        grid=(mid.shape[2] // sb,),
        in_specs=[rim, body, rim, body, pot_spec],
        out_specs=body,
        out_shape=jax.ShapeDtypeStruct(mid.shape, jnp.float32),
        scratch_shapes=[ext],
    )(left, mid, right, psi, pot)


def first_half_kernel(side_ref, rim_ref, mid_ref, pot_ref, out_ref, ext_ref):
    planes = mid_ref.shape[0]
    depth, ny = out_ref.shape[1], out_ref.shape[3]
    h = side_ref[0]
    ext_ref[pl.ds(reach, planes)] = mid_ref[...]
    ext_ref[pl.ds(h * (reach + planes), reach)] = rim_ref[...]
    base = h * (planes - reach)

    def body(x, carry):
        for z in range(depth):
            hv, mid = ham_planes(ext_ref, pot_ref, base + x, z, ny)
            out_ref[x, z] = (hv - center_shift * mid) / half_width
        return carry

    lax.fori_loop(0, planes - reach, body, 0)


def second_half_kernel(side_ref, rim_ref, a_ref, b_ref, psi_ref, pot_ref, out_ref, ext_ref):
    planes = psi_ref.shape[0]
    half = planes - reach
    depth, ny = out_ref.shape[1], out_ref.shape[3]
    h = side_ref[0]
    a_side = side_ref[1]
    ext_ref[pl.ds(reach + a_side * half, half)] = a_ref[...]
    ext_ref[pl.ds(reach + (1 - a_side) * half, half)] = b_ref[...]
    ext_ref[pl.ds(h * (reach + planes), reach)] = rim_ref[...]
    base = h * half

    def body(x, carry):
        for z in range(depth):
            hv, mid = ham_planes(ext_ref, pot_ref, base + x, z, ny)
            second = 2.0 / half_width * (hv - center_shift * mid) - psi_ref[base + x, z]
            out_ref[x, z] = second.astype(out_ref.dtype)
        return carry

    lax.fori_loop(0, half, body, 0)


def smem():
    return pl.BlockSpec(memory_space=pltpu.SMEM)


def whole(shape):
    return pl.BlockSpec(shape, lambda i: (0,) * len(shape))


def run_first_half(side, rim, mid, pot):
    planes, depth, states, ny = mid.shape
    half = (planes - reach, depth, states, ny)
    return pl.pallas_call(
        first_half_kernel,
        grid=(1,),
        in_specs=[smem(), whole(rim.shape), whole(mid.shape), whole(pot.shape)],
        out_specs=whole(half),
        out_shape=jax.ShapeDtypeStruct(half, jnp.float32),
        scratch_shapes=[pltpu.VMEM((planes + 2 * reach, depth, states, ny), jnp.float32)],
    )(side, rim, mid, pot)


def run_second_half(side, rim, a, b, psi, pot):
    planes, depth, states, ny = psi.shape
    return pl.pallas_call(
        second_half_kernel,
        grid=(1,),
        in_specs=[smem(), whole(rim.shape), whole(a.shape), whole(b.shape), whole(psi.shape), whole(pot.shape)],
        out_specs=whole(a.shape),
        out_shape=jax.ShapeDtypeStruct(a.shape, jnp.bfloat16),
        scratch_shapes=[pltpu.VMEM((planes + 2 * reach, depth, states, ny), jnp.float32)],
    )(side, rim, a, b, psi, pot)


def inner_outer(send_inner, send_outer):
    count = lax.axis_size("dom")
    inner = [(i, i + 1) if i % 2 == 0 else (i, i - 1) for i in range(count)]
    outer = [(i, (i - 1) % count) if i % 2 == 0 else (i, (i + 1) % count) for i in range(count)]
    return lax.ppermute(send_inner, "dom", inner), lax.ppermute(send_outer, "dom", outer)


def to_wire(second, parts):
    planes, depth, states, ny = second.shape
    chunk = planes * depth * ny // parts
    flat = second.astype(jnp.bfloat16).transpose(2, 0, 1, 3).reshape(states, parts, chunk)
    return flat.transpose(1, 0, 2).reshape(parts, states * chunk // ny, ny)


def per_device(psi, potential, rotation):
    own_states, planes, depth, ny = psi.shape
    psi_t = psi.transpose(1, 2, 0, 3)
    pot_t = potential[:, :, None, :]
    rows = planes * depth
    count = lax.axis_size("band")
    chunk = rows * ny // count
    wire = (count, own_states * chunk // ny, ny)
    if lax.axis_size("dom") % 2 or planes != 2 * reach or count % 2:
        left, right = swap_rims(psi_t[:reach], psi_t[planes - reach :])
        first, head, tail = run_first(left, psi_t, right, pot_t)
        left, right = swap_rims(head, tail)
        second = run_second(left, first, right, psi_t, pot_t)
        blocks = to_wire(second, count)
    else:
        even = lax.axis_index("dom") % 2 == 0
        hi = jnp.where(even, 1, 0).astype(jnp.int32)
        in_send = lax.dynamic_slice_in_dim(psi, hi * reach, reach, 1).transpose(1, 2, 0, 3)
        out_send = lax.dynamic_slice_in_dim(psi, (1 - hi) * reach, reach, 1).transpose(1, 2, 0, 3)
        psi_b, in_send, out_send = lax.optimization_barrier((psi, in_send, out_send))
        psi_t = psi_b.transpose(1, 2, 0, 3)
        rim_in, rim_out = inner_outer(in_send, out_send)
        part_a = run_first_half(hi.reshape(1), rim_in, psi_t, pot_t)
        _, rim_out = lax.optimization_barrier((part_a, rim_out))
        part_b = run_first_half((1 - hi).reshape(1), rim_out, psi_t, pot_t)
        rim_in, rim_out = inner_outer(part_a, part_b)
        sides_a = jnp.stack([hi, hi])
        sides_b = jnp.stack([1 - hi, hi])
        second_a = run_second_half(sides_a, rim_in, part_a, part_b, psi_t, pot_t)
        _, rim_out = lax.optimization_barrier((second_a, rim_out))
        second_b = run_second_half(sides_b, rim_out, part_a, part_b, psi_t, pot_t)
        wire_a = to_wire(second_a, count // 2)
        wire_b = to_wire(second_b, count // 2)
        blocks = jnp.where(
            even,
            jnp.concatenate([wire_b, wire_a], axis=0),
            jnp.concatenate([wire_a, wire_b], axis=0),
        )
    gathered = lax.all_to_all(blocks, "band", 0, 0, tiled=True)
    mixed = lax.dot_general(
        rotation,
        gathered.reshape(own_states * count, chunk),
        (((0,), (0,)), ((), ())),
        preferred_element_type=jnp.float32,
    ).astype(jnp.bfloat16)
    back = lax.all_to_all(mixed.reshape(wire), "band", 0, 0, tiled=True)
    result = back.reshape(count, own_states, chunk).transpose(1, 0, 2)
    return result.reshape(psi.shape)


def solution(mesh):
    in_specs = (P("band", "dom", None, None), P("dom", None, None), P())
    out_specs = P("band", "dom", None, None)
    return jax.shard_map(
        per_device, mesh=mesh, in_specs=in_specs, out_specs=out_specs, check_vma=False
    )
```

```python
import jax
import jax.numpy as jnp
from jax import lax
from jax.experimental import pallas as pl
from jax.experimental.pallas import tpu as pltpu
from jax.sharding import PartitionSpec as P

coeffs = (
    -5369.0 / 1800.0,
    12.0 / 7.0,
    -15.0 / 56.0,
    10.0 / 189.0,
    -1.0 / 112.0,
    2.0 / 1925.0,
    -1.0 / 16632.0,
)
center_shift = 32.5
half_width = 27.5
reach = 6
state_block = 32


def swap_rims(head, tail):
    count = lax.axis_size("dom")
    if count % 2:
        left = lax.ppermute(tail, "dom", [(i, (i + 1) % count) for i in range(count)])
        right = lax.ppermute(head, "dom", [((i + 1) % count, i) for i in range(count)])
        return left, right
    even = lax.axis_index("dom") % 2 == 0
    inner = [(i, i + 1) if i % 2 == 0 else (i, i - 1) for i in range(count)]
    outer = [(i, (i - 1) % count) if i % 2 == 0 else (i, (i + 1) % count) for i in range(count)]
    got_inner = lax.ppermute(jnp.where(even, tail, head), "dom", inner)
    got_outer = lax.ppermute(jnp.where(even, head, tail), "dom", outer)
    left = jnp.where(even, got_outer, got_inner)
    right = jnp.where(even, got_inner, got_outer)
    return left, right


def ham_planes(ext_ref, pot_ref, x, z, ny):
    mid = ext_ref[x + reach, z]
    lap = (3.0 * coeffs[0]) * mid
    for k in range(1, 7):
        lap = lap + coeffs[k] * (ext_ref[x + reach + k, z] + ext_ref[x + reach - k, z])
    for k in range(1, 7):
        lap = lap + coeffs[k] * (pltpu.roll(mid, k, 1) + pltpu.roll(mid, ny - k, 1))
    lap = lap + coeffs[1] * ext_ref[x + reach, 1 - z]
    return -2.0 * lap + pot_ref[x, z] * mid, mid


def fill_ext(left_ref, mid_ref, right_ref, ext_ref):
    planes = mid_ref.shape[0]
    ext_ref[pl.ds(0, reach)] = left_ref[...]
    ext_ref[pl.ds(reach, planes)] = mid_ref[...]
    ext_ref[pl.ds(reach + planes, reach)] = right_ref[...]


def first_kernel(left_ref, mid_ref, right_ref, pot_ref, out_ref, head_ref, tail_ref, ext_ref):
    planes, depth, _, ny = out_ref.shape
    fill_ext(left_ref, mid_ref, right_ref, ext_ref)

    def body(x, carry):
        for z in range(depth):
            h, mid = ham_planes(ext_ref, pot_ref, x, z, ny)
            out_ref[x, z] = (h - center_shift * mid) / half_width
        return carry

    lax.fori_loop(0, planes, body, 0)
    head_ref[...] = out_ref[pl.ds(0, reach)]
    tail_ref[...] = out_ref[pl.ds(planes - reach, reach)]


def second_kernel(left_ref, mid_ref, right_ref, psi_ref, pot_ref, out_ref, ext_ref):
    planes, depth, _, ny = out_ref.shape
    fill_ext(left_ref, mid_ref, right_ref, ext_ref)

    def body(x, carry):
        for z in range(depth):
            h, mid = ham_planes(ext_ref, pot_ref, x, z, ny)
            out_ref[x, z] = 2.0 / half_width * (h - center_shift * mid) - psi_ref[x, z]
        return carry

    lax.fori_loop(0, planes, body, 0)


def specs(mid, sb):
    planes, depth, _, ny = mid.shape
    rim = pl.BlockSpec((reach, depth, sb, ny), lambda i: (0, 0, i, 0))
    body = pl.BlockSpec((planes, depth, sb, ny), lambda i: (0, 0, i, 0))
    pot = pl.BlockSpec((planes, depth, 1, ny), lambda i: (0, 0, 0, 0))
    ext = pltpu.VMEM((planes + 2 * reach, depth, sb, ny), jnp.float32)
    return rim, body, pot, ext


def run_first(left, mid, right, pot):
    sb = state_block
    rim, body, pot_spec, ext = specs(mid, sb)
    return pl.pallas_call(
        first_kernel,
        grid=(mid.shape[2] // sb,),
        in_specs=[rim, body, rim, pot_spec],
        out_specs=[body, rim, rim],
        out_shape=[
            jax.ShapeDtypeStruct(mid.shape, jnp.float32),
            jax.ShapeDtypeStruct(left.shape, jnp.float32),
            jax.ShapeDtypeStruct(left.shape, jnp.float32),
        ],
        scratch_shapes=[ext],
    )(left, mid, right, pot)


def run_second(left, mid, right, psi, pot):
    sb = state_block
    rim, body, pot_spec, ext = specs(mid, sb)
    return pl.pallas_call(
        second_kernel,
        grid=(mid.shape[2] // sb,),
        in_specs=[rim, body, rim, body, pot_spec],
        out_specs=body,
        out_shape=jax.ShapeDtypeStruct(mid.shape, jnp.float32),
        scratch_shapes=[ext],
    )(left, mid, right, psi, pot)


def first_half_kernel(side_ref, rim_ref, mid_ref, pot_ref, out_ref, ext_ref):
    planes = mid_ref.shape[0]
    depth, ny = out_ref.shape[1], out_ref.shape[3]
    h = side_ref[0]
    ext_ref[pl.ds(reach, planes)] = mid_ref[...]
    ext_ref[pl.ds(h * (reach + planes), reach)] = rim_ref[...]
    base = h * (planes - reach)

    def body(x, carry):
        for z in range(depth):
            hv, mid = ham_planes(ext_ref, pot_ref, base + x, z, ny)
            out_ref[x, z] = (hv - center_shift * mid) / half_width
        return carry

    lax.fori_loop(0, planes - reach, body, 0)


def second_half_kernel(side_ref, rim_ref, a_ref, b_ref, psi_ref, pot_ref, out_ref, ext_ref):
    half = a_ref.shape[0]
    planes = 2 * half
    depth, ny = out_ref.shape[1], out_ref.shape[3]
    h = side_ref[0]
    a_side = side_ref[1]
    ext_ref[pl.ds(reach + a_side * half, half)] = a_ref[...]
    ext_ref[pl.ds(reach + (1 - a_side) * half, half)] = b_ref[...]
    ext_ref[pl.ds(h * (reach + planes), reach)] = rim_ref[...]
    base = h * half

    def body(x, carry):
        for z in range(depth):
            hv, mid = ham_planes(ext_ref, pot_ref, base + x, z, ny)
            second = 2.0 / half_width * (hv - center_shift * mid) - psi_ref[x, z]
            out_ref[x, z] = second.astype(out_ref.dtype)
        return carry

    lax.fori_loop(0, half, body, 0)


def smem():
    return pl.BlockSpec(memory_space=pltpu.SMEM)


def whole(shape):
    return pl.BlockSpec(shape, lambda i: (0,) * len(shape))


def run_first_half(side, rim, mid, pot):
    planes, depth, states, ny = mid.shape
    half = (planes - reach, depth, states, ny)
    return pl.pallas_call(
        first_half_kernel,
        grid=(1,),
        in_specs=[smem(), whole(rim.shape), whole(mid.shape), whole(pot.shape)],
        out_specs=whole(half),
        out_shape=jax.ShapeDtypeStruct(half, jnp.float32),
        scratch_shapes=[pltpu.VMEM((planes + 2 * reach, depth, states, ny), jnp.float32)],
    )(side, rim, mid, pot)


def run_second_half(side, rim, a, b, psi, pot):
    depth, states, ny = psi.shape[1:]
    planes = 2 * a.shape[0]
    return pl.pallas_call(
        second_half_kernel,
        grid=(1,),
        in_specs=[smem(), whole(rim.shape), whole(a.shape), whole(b.shape), whole(psi.shape), whole(pot.shape)],
        out_specs=whole(a.shape),
        out_shape=jax.ShapeDtypeStruct(a.shape, jnp.bfloat16),
        scratch_shapes=[pltpu.VMEM((planes + 2 * reach, depth, states, ny), jnp.float32)],
    )(side, rim, a, b, psi, pot)


def inner_outer(send_inner, send_outer):
    count = lax.axis_size("dom")
    inner = [(i, i + 1) if i % 2 == 0 else (i, i - 1) for i in range(count)]
    outer = [(i, (i - 1) % count) if i % 2 == 0 else (i, (i + 1) % count) for i in range(count)]
    return lax.ppermute(send_inner, "dom", inner), lax.ppermute(send_outer, "dom", outer)


def to_wire(second, parts):
    planes, depth, states, ny = second.shape
    chunk = planes * depth * ny // parts
    flat = second.astype(jnp.bfloat16).transpose(2, 0, 1, 3).reshape(states, parts, chunk)
    return flat.transpose(1, 0, 2).reshape(parts, states * chunk // ny, ny)


def per_device(psi, potential, rotation):
    own_states, planes, depth, ny = psi.shape
    psi_t = psi.transpose(1, 2, 0, 3)
    pot_t = potential[:, :, None, :]
    rows = planes * depth
    count = lax.axis_size("band")
    chunk = rows * ny // count
    wire = (count, own_states * chunk // ny, ny)
    if lax.axis_size("dom") % 2 or planes != 2 * reach or count % 2:
        left, right = swap_rims(psi_t[:reach], psi_t[planes - reach :])
        first, head, tail = run_first(left, psi_t, right, pot_t)
        left, right = swap_rims(head, tail)
        second = run_second(left, first, right, psi_t, pot_t)
        blocks = to_wire(second, count)
    else:
        even = lax.axis_index("dom") % 2 == 0
        hi = jnp.where(even, 1, 0).astype(jnp.int32)
        head, tail = psi_t[:reach], psi_t[planes - reach :]
        rim_in, rim_out = inner_outer(jnp.where(even, tail, head), jnp.where(even, head, tail))
        part_a = run_first_half(hi.reshape(1), rim_in, psi_t, pot_t)
        _, rim_out = lax.optimization_barrier((part_a, rim_out))
        part_b = run_first_half((1 - hi).reshape(1), rim_out, psi_t, pot_t)
        rim_in, rim_out = inner_outer(part_a, part_b)
        sides_a = jnp.stack([hi, hi])
        sides_b = jnp.stack([1 - hi, hi])
        psi_a = lax.dynamic_slice_in_dim(psi_t, hi * reach, reach, 0)
        psi_b = lax.dynamic_slice_in_dim(psi_t, (1 - hi) * reach, reach, 0)
        second_a = run_second_half(sides_a, rim_in, part_a, part_b, psi_a, pot_t)
        _, rim_out = lax.optimization_barrier((second_a, rim_out))
        second_b = run_second_half(sides_b, rim_out, part_a, part_b, psi_b, pot_t)
        wire_a = to_wire(second_a, count // 2)
        wire_b = to_wire(second_b, count // 2)
        blocks = jnp.where(
            even,
            jnp.concatenate([wire_b, wire_a], axis=0),
            jnp.concatenate([wire_a, wire_b], axis=0),
        )
    gathered = lax.all_to_all(blocks, "band", 0, 0, tiled=True)
    mixed = lax.dot_general(
        rotation,
        gathered.reshape(own_states * count, chunk),
        (((0,), (0,)), ((), ())),
        preferred_element_type=jnp.float32,
    ).astype(jnp.bfloat16)
    back = lax.all_to_all(mixed.reshape(wire), "band", 0, 0, tiled=True)
    result = back.reshape(count, own_states, chunk).transpose(1, 0, 2)
    return result.reshape(psi.shape)


def solution(mesh):
    in_specs = (P("band", "dom", None, None), P("dom", None, None), P())
    out_specs = P("band", "dom", None, None)
    return jax.shard_map(
        per_device, mesh=mesh, in_specs=in_specs, out_specs=out_specs, check_vma=False
    )
```
